32 devices in a mesh: grp: 4 (over y, core), col: 8 (over z, x).
Axes of the slice: x: 2, y: 2, z: 4, core: 2. Of those that a mesh axis runs over, the one named last changes fastest.
Arguments:
- orbitals: float32 [32, 14336], P('grp', 'col'), may hold values from -6 to 6
- column_cell: int32 [448], replicated, may hold values from 0 to 2303, as said below
- column_length: int32 [448], replicated, may hold values from 1 to 32, as said below
- sources: int32 [3], replicated, may hold values from 0 to 31, as said below
- weights: float32 [3], replicated, may hold values from 0.5 to 2
Outputs:
- exchange_coefficients: float32 [32, 14336], P('grp', 'col')
The draws below stay inside these ranges and needn't reach their ends.
Inputs may be any that keep to these rules, and one draw needn't show every extreme that they name: `column_cell`: the cells are distinct and are the 448 cells of smallest f(a)^2 + f(b)^2, f(k) = min(k, 48 - k), so they fill a disk around zero frequency. `column_length`: lengths fall from the centre of the disk to its rim like chords of a sphere; the centre column has 32 live slots and the outermost has 1. `sources`: distinct band indices.
All inputs are finite; a program needn't handle non-finite values.
Results may differ from the reference program's by a relative error of at most 0.0003.
Values sent between devices are 32-bit elements; how exact they have to be, the bound alone decides.
No kernel may reach another device: no remote copies, remote signals or barrier semaphores. Data moves between devices by JAX's collectives and lax.ppermute only.
A program may use at most 64 MiB of HBM per device.

```python
import math
import jax
import jax.numpy as jnp
from jax import lax

GRID = 48
DEPTH = 32
SRC = 3
BANDS = 32
COLUMNS = 448


def int_root(value):
    result = jnp.zeros_like(value)
    for bit in reversed(range(15)):
        trial = result + (1 << bit)
        result = jnp.where(trial * trial <= value, trial, result)
    return result


def sphere_columns(key):
    first, second = jax.random.split(jax.random.fold_in(key, 7))
    cell = jnp.arange(GRID * GRID, dtype=jnp.int32)
    row_freq = jnp.minimum(cell // GRID, GRID - cell // GRID)
    col_freq = jnp.minimum(cell % GRID, GRID - cell % GRID)
    radius_sq = row_freq * row_freq + col_freq * col_freq
    rank = jax.random.permutation(first, GRID * GRID).astype(jnp.int32)
    scores = radius_sq * (GRID * GRID) + rank
    chosen = jnp.argsort(scores, stable=True)[:COLUMNS].astype(jnp.int32)
    shuffle = jax.random.permutation(second, COLUMNS).astype(jnp.int32)
    cells = chosen[shuffle]
    chosen_sq = radius_sq[cells]
    outer_sq = jnp.max(chosen_sq)
    scale_num = int_root(65536 * (outer_sq - chosen_sq))
    scale_den = int_root(65536 * outer_sq + 0 * chosen_sq)
    lengths = 1 + (DEPTH - 1) * scale_num // scale_den
    return (cells.astype(jnp.int32), lengths.astype(jnp.int32))


def draw_column_cell(key, part):
    return sphere_columns(key)[0]


def draw_column_length(key, part):
    return sphere_columns(key)[1]


def draw_sources(key, part):
    first, second = jax.random.split(key)
    inner = jax.random.permutation(first, BANDS - 2)[:SRC - 2] + 1
    ends = jnp.array([0, BANDS - 1], dtype=jnp.int32)
    picked = jnp.concatenate([ends, inner.astype(jnp.int32)])
    return jax.random.permutation(second, picked).astype(jnp.int32)


def shard_levels(stream_key, shape, pieces, smallest, largest):
    loudness, own = 1.0, jax.random.fold_in(stream_key, 6)
    for axis_at, shards_of in pieces:
        draws = jnp.exp(jax.random.uniform(jax.random.fold_in(own, axis_at), (shards_of,), jnp.float32, smallest / len(pieces), largest / len(pieces)))
        loudness = loudness * jnp.repeat(draws, shape[axis_at] // shards_of).reshape([-1 if axis == axis_at else 1 for axis in range(len(shape))])
    return loudness


def scatter_about(key, dims, deviation, most, cuts=(), kind=jnp.bfloat16):
    level = shard_levels(key, dims, cuts, -0.22, 0.18) if cuts else 1.0
    drawn = jax.random.normal(key, dims, jnp.float32) * deviation * level
    return jnp.minimum(jnp.maximum(drawn, -most), most).astype(kind)


def setup_inputs(seed: int = 0) -> dict:
    keys = jax.random.split(jax.random.key(seed), 6)
    return {
        "orbitals": scatter_about(keys[0], (BANDS, COLUMNS * DEPTH), 1.0, 6.0, ((0, 4), (1, 8)), jnp.float32),
        "column_cell": draw_column_cell(jax.random.fold_in(keys[5], 71), 0),
        "column_length": draw_column_length(jax.random.fold_in(keys[5], 71), 0),
        "sources": draw_sources(jax.random.fold_in(keys[5], 71), 0),
        "weights": jnp.clip(jax.random.uniform(keys[4], (SRC,), jnp.float32, 0.5, 2.0), 0.5, 2.0),
    }


kernel_scale = 20000.0
screen_shift = 4.0

def cas_matrix(extent):
    index = jnp.arange(extent, dtype=jnp.int32)
    phase = index[:, None] * index[None, :] % extent
    angle = phase.astype(jnp.float32) * (2.0 * math.pi / extent)
    return (jnp.cos(angle) + jnp.sin(angle)) / math.sqrt(extent)

def kernel_grid(extent):
    index = jnp.arange(extent, dtype=jnp.int32)
    freq = jnp.minimum(index, extent - index)
    square = freq * freq
    total = square[:, None, None] + square[None, :, None] + square[None, None, :]
    kernel = kernel_scale / (total.astype(jnp.float32) + screen_shift)
    return jnp.where(total > 0, kernel, 0.0)

def slot_frequency(column_length, depth, extent):
    slot = jnp.arange(depth, dtype=jnp.int32)
    shift = slot[None, :] - column_length[:, None] // 2
    live = (slot[None, :] < column_length[:, None]).astype(jnp.int32)
    return (shift % extent, live)

def plane_axes(field, table):
    field = jnp.einsum('ka,abc->kbc', table, field, precision=lax.Precision.HIGHEST)
    return jnp.einsum('kb,abc->akc', table, field, precision=lax.Precision.HIGHEST)

def cas_three(field, table):
    field = plane_axes(field, table)
    return jnp.einsum('abc,ck->abk', field, table, precision=lax.Precision.HIGHEST)

def to_grid(coeff_row, column_cell, freq, live, table, extent):
    count, depth = freq.shape
    values = jnp.where(live > 0, coeff_row.reshape(count, depth), 0.0)
    rows = jnp.broadcast_to(jnp.arange(count, dtype=jnp.int32)[:, None], (count, depth))
    spread = jnp.zeros((count, extent), jnp.float32).at[rows, freq].set(values)
    columns = jnp.dot(spread, table, precision=lax.Precision.HIGHEST)
    plane = jnp.zeros((extent * extent, extent), jnp.float32).at[column_cell].set(columns)
    return plane_axes(plane.reshape(extent, extent, extent), table)

def from_grid(field, column_cell, freq, live, table, extent):
    field = plane_axes(field, table)
    columns = field.reshape(extent * extent, extent)[column_cell]
    columns = jnp.dot(columns, table, precision=lax.Precision.HIGHEST)
    picked = jnp.take_along_axis(columns, freq, axis=1)
    return jnp.where(live > 0, picked, 0.0).reshape(-1)

def reference(orbitals, column_cell, column_length, sources, weights):
    table = cas_matrix(GRID)
    kernel = kernel_grid(GRID)
    freq, live = slot_frequency(column_length, DEPTH, GRID)
    source_grids = [to_grid(orbitals[sources[j]], column_cell, freq, live, table, GRID) for j in range(SRC)]

    def one_band(row):
        own = to_grid(row, column_cell, freq, live, table, GRID)
        total = jnp.zeros_like(own)
        for j in range(SRC):
            density = own * source_grids[j]
            potential = cas_three(kernel * cas_three(density, table), table)
            total = total + weights[j] * potential * source_grids[j]
        return -from_grid(total, column_cell, freq, live, table, GRID)
    return lax.map(one_band, orbitals)
```

```python
import math

import jax
import jax.numpy as jnp
from jax import lax
from jax.sharding import PartitionSpec as P

GRID = 48

kernel_scale = 20000.0
screen_shift = 4.0

HI = lax.Precision.HIGHEST


def cas_matrix(extent):
    index = jnp.arange(extent, dtype=jnp.int32)
    phase = index[:, None] * index[None, :] % extent
    angle = phase.astype(jnp.float32) * (2.0 * math.pi / extent)
    return (jnp.cos(angle) + jnp.sin(angle)) / math.sqrt(extent)


def kernel_grid(extent):
    index = jnp.arange(extent, dtype=jnp.int32)
    freq = jnp.minimum(index, extent - index)
    square = freq * freq
    total = square[:, None, None] + square[None, :, None] + square[None, None, :]
    kernel = kernel_scale / (total.astype(jnp.float32) + screen_shift)
    return jnp.where(total > 0, kernel, 0.0)


def slot_table(column_length, depth, table, extent):
    slot = jnp.arange(depth, dtype=jnp.int32)
    freq = (slot[None, :] - column_length[:, None] // 2) % extent
    live = slot[None, :] < column_length[:, None]
    hot = (freq[:, :, None] == jnp.arange(extent, dtype=jnp.int32)[None, None, :]) & live[:, :, None]
    hot = hot.astype(jnp.float32).reshape(-1, extent)
    gt = jnp.dot(hot, table, precision=HI)
    return gt.reshape(column_length.shape[0], depth, extent)


def plane_matrix(column_cell, table, extent):
    index = jnp.arange(extent, dtype=jnp.int32)
    first = (column_cell[None, :] // extent == index[:, None]).astype(jnp.float32)
    second = (column_cell[None, :] % extent == index[:, None]).astype(jnp.float32)
    ta = jnp.dot(table, first, precision=HI)
    tb = jnp.dot(table, second, precision=HI)
    return (ta[:, None, :] * tb[None, :, :]).reshape(extent * extent, -1)


def cas_three(field, table):
    field = jnp.einsum("nabc,ck->nabk", field, table, precision=HI)
    field = jnp.einsum("nabc,kb->nakc", field, table, precision=HI)
    return jnp.einsum("nabc,ka->nkbc", field, table, precision=HI)


def make_local(n_grp_bands, n_col):
    def local(orbitals, column_cell, column_length, sources, weights):
        extent = GRID
        count = column_cell.shape[0]
        depth = orbitals.shape[1] * n_col // count
        table = cas_matrix(extent)
        kernel = kernel_grid(extent)
        gt = slot_table(column_length, depth, table, extent)
        w = plane_matrix(column_cell, table, extent)

        own_row = lax.all_to_all(orbitals, "col", split_axis=0, concat_axis=1, tiled=True)
        g = lax.axis_index("grp")
        owner = sources // n_grp_bands
        picked = orbitals[sources % n_grp_bands]
        picked = jnp.where((owner == g)[:, None], picked, 0.0)
        picked = lax.psum(picked, "grp")
        src_rows = lax.all_gather(picked, "col", axis=1, tiled=True)

        rows = jnp.concatenate([own_row, src_rows], axis=0)
        n = rows.shape[0]
        coeff = rows.reshape(n, count, depth)
        cols = jnp.einsum("nct,ctk->nck", coeff, gt, precision=HI)
        grids = jnp.einsum("pc,nck->npk", w, cols, precision=HI)
        grids = grids.reshape(n, extent, extent, extent)
        own = grids[:1]
        src = grids[1:]
        density = own * src
        potential = cas_three(kernel[None] * cas_three(density, table), table)
        total = jnp.sum(weights[:, None, None, None] * potential * src, axis=0)
        back = jnp.einsum("pc,pk->ck", w, total.reshape(extent * extent, extent), precision=HI)
        out = -jnp.einsum("ck,ctk->ct", back, gt, precision=HI)
        return lax.all_to_all(out.reshape(1, -1), "col", split_axis=1, concat_axis=0, tiled=True)

    return local


def solution(mesh):
    n_grp = mesh.shape["grp"]
    n_col = mesh.shape["col"]

    def run(orbitals, column_cell, column_length, sources, weights):
        n_grp_bands = orbitals.shape[0] // n_grp
        body = make_local(n_grp_bands, n_col)
        return jax.shard_map(
            body,
            mesh=mesh,
            in_specs=(P("grp", "col"), P(), P(), P(), P()),
            out_specs=P("grp", "col"),
            check_vma=False,
        )(orbitals, column_cell, column_length, sources, weights)

    return run
```

```python
import math

import jax
import jax.numpy as jnp
from jax import lax
from jax.sharding import PartitionSpec as P

GRID = 48

kernel_scale = 20000.0
screen_shift = 4.0

HI = lax.Precision.HIGHEST


def cas_matrix(extent):
    index = jnp.arange(extent, dtype=jnp.int32)
    phase = index[:, None] * index[None, :] % extent
    angle = phase.astype(jnp.float32) * (2.0 * math.pi / extent)
    return (jnp.cos(angle) + jnp.sin(angle)) / math.sqrt(extent)


def kernel_grid(extent):
    index = jnp.arange(extent, dtype=jnp.int32)
    freq = jnp.minimum(index, extent - index)
    square = freq * freq
    total = square[:, None, None] + square[None, :, None] + square[None, None, :]
    kernel = kernel_scale / (total.astype(jnp.float32) + screen_shift)
    return jnp.where(total > 0, kernel, 0.0)


def shift_tables(column_length, depth, extent):
    half = column_length // 2
    index = jnp.arange(extent, dtype=jnp.int32)
    phase = (half[:, None] * index[None, :]) % extent
    angle = phase.astype(jnp.float32) * (2.0 * math.pi / extent)
    slot = jnp.arange(depth, dtype=jnp.int32)
    live = slot[None, :] < column_length[:, None]
    return jnp.cos(angle), jnp.sin(angle), live


def plane_matrix(column_cell, table, extent):
    index = jnp.arange(extent, dtype=jnp.int32)
    first = (column_cell[None, :] // extent == index[:, None]).astype(jnp.float32)
    second = (column_cell[None, :] % extent == index[:, None]).astype(jnp.float32)
    ta = jnp.dot(table, first, precision=HI)
    tb = jnp.dot(table, second, precision=HI)
    return (ta[:, None, :] * tb[None, :, :]).reshape(extent * extent, -1)


def cas_three(field, table):
    field = jnp.einsum("absc,ck->absk", field, table, precision=HI)
    field = jnp.einsum("absc,kb->aksc", field, table, precision=HI)
    return jnp.einsum("absc,ka->kbsc", field, table, precision=HI)


def make_local(n_grp_bands, n_grp, n_col):
    def local(orbitals, column_cell, column_length, sources, weights):
        extent = GRID
        count = column_cell.shape[0]
        width = orbitals.shape[1]
        depth = width * n_col // count
        n_src = sources.shape[0]
        table = cas_matrix(extent)
        kernel = kernel_grid(extent)
        cos_h, sin_h, live = shift_tables(column_length, depth, extent)
        slot = jnp.arange(depth, dtype=jnp.int32)
        fwd = jnp.concatenate([table[:depth], table[(extent - slot) % extent]], axis=1)
        bwd = jnp.concatenate([table[:, :depth], table[:, (extent - slot) % extent]], axis=0)
        w = lax.optimization_barrier(plane_matrix(column_cell, table, extent))

        g = lax.axis_index("grp")
        owner = sources // n_grp_bands
        picked = orbitals[sources % n_grp_bands]
        picked = jnp.where((owner == g)[:, None], picked, 0.0)
        spread = jnp.broadcast_to(picked[None], (n_grp, n_src, width))
        picked = jnp.sum(lax.all_to_all(spread, "grp", 0, 0, tiled=True), axis=0)
        send = jnp.concatenate(
            [orbitals[:, None, :], jnp.broadcast_to(picked[None], (n_grp_bands, n_src, width))], axis=1)
        got = lax.all_to_all(send, "col", 0, 0, tiled=True)
        n = 1 + n_src
        coeff = got.reshape(n_col, n, width // depth, depth).transpose(0, 2, 1, 3).reshape(count, n, depth)
        coeff = jnp.where(live[:, None, :], coeff, 0.0)
        both = jnp.dot(coeff.reshape(count * n, depth), fwd, precision=HI).reshape(count, n, 2, extent)
        cols = cos_h[:, None, :] * both[:, :, 0] - sin_h[:, None, :] * both[:, :, 1]
        grids = jnp.dot(w, cols.reshape(count, n * extent), precision=HI)
        grids = grids.reshape(extent, extent, n, extent)
        own = grids[:, :, :1]
        src = grids[:, :, 1:]
        density = own * src
        potential = cas_three(kernel[:, :, None, :] * cas_three(density, table), table)
        total = jnp.sum(weights[None, None, :, None] * potential * src, axis=2)
        back = lax.dot_general(w, total.reshape(extent * extent, extent), (((0,), (0,)), ((), ())), precision=HI)
        scaled = jnp.concatenate([back * cos_h, -(back * sin_h)], axis=1)
        out = -jnp.dot(scaled, bwd, precision=HI)
        out = jnp.where(live, out, 0.0)
        return lax.all_to_all(out.reshape(n_col, 1, width), "col", 0, 0, tiled=True).reshape(n_col, width)

    return local


def solution(mesh):
    n_grp = mesh.shape["grp"]
    n_col = mesh.shape["col"]

    def run(orbitals, column_cell, column_length, sources, weights):
        n_grp_bands = orbitals.shape[0] // n_grp
        body = make_local(n_grp_bands, n_grp, n_col)
        return jax.shard_map(
            body,
            mesh=mesh,
            in_specs=(P("grp", "col"), P(), P(), P(), P()),
            out_specs=P("grp", "col"),
            check_vma=False,
        )(orbitals, column_cell, column_length, sources, weights)

    return run
```

```python
import math

import jax
import jax.numpy as jnp
from jax import lax
from jax.sharding import PartitionSpec as P

GRID = 48

kernel_scale = 20000.0
screen_shift = 4.0

HI = lax.Precision.HIGHEST
MID = lax.Precision.HIGH


def cas_matrix(extent):
    index = jnp.arange(extent, dtype=jnp.int32)
    phase = index[:, None] * index[None, :] % extent
    angle = phase.astype(jnp.float32) * (2.0 * math.pi / extent)
    return (jnp.cos(angle) + jnp.sin(angle)) / math.sqrt(extent)


def kernel_grid(extent):
    index = jnp.arange(extent, dtype=jnp.int32)
    freq = jnp.minimum(index, extent - index)
    square = freq * freq
    total = square[:, None, None] + square[None, :, None] + square[None, None, :]
    kernel = kernel_scale / (total.astype(jnp.float32) + screen_shift)
    return jnp.where(total > 0, kernel, 0.0)


def shift_tables(column_length, depth, extent):
    half = column_length // 2
    index = jnp.arange(extent, dtype=jnp.int32)
    phase = (half[:, None] * index[None, :]) % extent
    angle = phase.astype(jnp.float32) * (2.0 * math.pi / extent)
    slot = jnp.arange(depth, dtype=jnp.int32)
    live = slot[None, :] < column_length[:, None]
    return jnp.cos(angle), jnp.sin(angle), live


def plane_matrix(column_cell, table, extent):
    index = jnp.arange(extent, dtype=jnp.int32)
    first = (column_cell[None, :] // extent == index[:, None]).astype(jnp.float32)
    second = (column_cell[None, :] % extent == index[:, None]).astype(jnp.float32)
    ta = jnp.dot(table, first, precision=HI)
    tb = jnp.dot(table, second, precision=HI)
    return (ta[:, None, :] * tb[None, :, :]).reshape(extent * extent, -1)


def cas_three(field, table):
    field = jnp.einsum("absc,ck->absk", field, table, precision=MID)
    field = jnp.einsum("absc,kb->aksc", field, table, precision=MID)
    return jnp.einsum("absc,ka->kbsc", field, table, precision=MID)


def make_local(n_grp_bands, n_grp, n_col):
    def local(orbitals, column_cell, column_length, sources, weights):
        extent = GRID
        count = column_cell.shape[0]
        width = orbitals.shape[1]
        depth = width * n_col // count
        n_src = sources.shape[0]
        table = cas_matrix(extent)
        kernel = kernel_grid(extent)
        cos_h, sin_h, live = shift_tables(column_length, depth, extent)
        slot = jnp.arange(depth, dtype=jnp.int32)
        fwd = jnp.concatenate([table[:depth], table[(extent - slot) % extent]], axis=1)
        bwd = jnp.concatenate([table[:, :depth], table[:, (extent - slot) % extent]], axis=0)
        w = lax.optimization_barrier(plane_matrix(column_cell, table, extent))

        g = lax.axis_index("grp")
        owner = sources // n_grp_bands
        picked = orbitals[sources % n_grp_bands]
        picked = jnp.where((owner == g)[:, None], picked, 0.0)
        spread = jnp.broadcast_to(picked[None], (n_grp, n_src, width))
        picked = jnp.sum(lax.all_to_all(spread, "grp", 0, 0, tiled=True), axis=0)
        send = jnp.concatenate(
            [orbitals[:, None, :], jnp.broadcast_to(picked[None], (n_grp_bands, n_src, width))], axis=1)
        got = lax.all_to_all(send, "col", 0, 0, tiled=True)
        n = 1 + n_src
        coeff = got.reshape(n_col, n, width // depth, depth).transpose(0, 2, 1, 3).reshape(count, n, depth)
        coeff = jnp.where(live[:, None, :], coeff, 0.0)
        both = jnp.dot(coeff.reshape(count * n, depth), fwd, precision=MID).reshape(count, n, 2, extent)
        cols = cos_h[:, None, :] * both[:, :, 0] - sin_h[:, None, :] * both[:, :, 1]
        grids = jnp.dot(w, cols.reshape(count, n * extent), precision=MID)
        grids = grids.reshape(extent, extent, n, extent)
        own = grids[:, :, :1]
        src = grids[:, :, 1:]
        density = own * src
        potential = cas_three(kernel[:, :, None, :] * cas_three(density, table), table)
        total = jnp.sum(weights[None, None, :, None] * potential * src, axis=2)
        back = lax.dot_general(w, total.reshape(extent * extent, extent), (((0,), (0,)), ((), ())), precision=MID)
        scaled = jnp.concatenate([back * cos_h, -(back * sin_h)], axis=1)
        out = -jnp.dot(scaled, bwd, precision=MID)
        out = jnp.where(live, out, 0.0)
        return lax.all_to_all(out.reshape(n_col, 1, width), "col", 0, 0, tiled=True).reshape(n_col, width)

    return local


def solution(mesh):
    n_grp = mesh.shape["grp"]
    n_col = mesh.shape["col"]

    def run(orbitals, column_cell, column_length, sources, weights):
        n_grp_bands = orbitals.shape[0] // n_grp
        body = make_local(n_grp_bands, n_grp, n_col)
        return jax.shard_map(
            body,
            mesh=mesh,
            in_specs=(P("grp", "col"), P(), P(), P(), P()),
            out_specs=P("grp", "col"),
            check_vma=False,
        )(orbitals, column_cell, column_length, sources, weights)

    return run
```

```python
import math

import jax
import jax.numpy as jnp
from jax import lax
from jax.sharding import PartitionSpec as P

GRID = 48

kernel_scale = 20000.0
screen_shift = 4.0

HI = lax.Precision.HIGHEST
MID = lax.Precision.HIGH


def cas_matrix(extent):
    index = jnp.arange(extent, dtype=jnp.int32)
    phase = index[:, None] * index[None, :] % extent
    angle = phase.astype(jnp.float32) * (2.0 * math.pi / extent)
    return (jnp.cos(angle) + jnp.sin(angle)) / math.sqrt(extent)


def kernel_grid(extent):
    index = jnp.arange(extent, dtype=jnp.int32)
    freq = jnp.minimum(index, extent - index)
    square = freq * freq
    total = square[:, None, None] + square[None, :, None] + square[None, None, :]
    kernel = kernel_scale / (total.astype(jnp.float32) + screen_shift)
    return jnp.where(total > 0, kernel, 0.0)


def shift_tables(column_length, depth, extent):
    half = column_length // 2
    index = jnp.arange(extent, dtype=jnp.int32)
    phase = (half[:, None] * index[None, :]) % extent
    angle = phase.astype(jnp.float32) * (2.0 * math.pi / extent)
    slot = jnp.arange(depth, dtype=jnp.int32)
    live = slot[None, :] < column_length[:, None]
    return jnp.cos(angle), jnp.sin(angle), live


def plane_matrix(column_cell, table, extent):
    index = jnp.arange(extent, dtype=jnp.int32)
    first = (column_cell[None, :] // extent == index[:, None]).astype(jnp.float32)
    second = (column_cell[None, :] % extent == index[:, None]).astype(jnp.float32)
    ta = jnp.dot(table, first, precision=HI)
    tb = jnp.dot(table, second, precision=HI)
    return (ta[:, None, :] * tb[None, :, :]).reshape(extent * extent, -1)


def cas_three(field, table):
    field = jnp.einsum("absc,ck->absk", field, table, precision=MID)
    field = jnp.einsum("absc,kb->aksc", field, table, precision=MID)
    return jnp.einsum("absc,ka->kbsc", field, table, precision=MID)


def exchange(blocks, axis, size):
    me = lax.axis_index(axis)
    got = [blocks[me]]
    for shift in range(1, size):
        part = lax.dynamic_index_in_dim(blocks, (me + shift) % size, 0, keepdims=False)
        perm = [(i, (i + shift) % size) for i in range(size)]
        got.append(lax.ppermute(part, axis, perm))
    got = jnp.stack(got)
    order = (me - jnp.arange(size, dtype=jnp.int32)) % size
    return got[order]


def make_local(n_grp_bands, n_grp, n_col):
    def local(orbitals, column_cell, column_length, sources, weights):
        extent = GRID
        count = column_cell.shape[0]
        width = orbitals.shape[1]
        depth = width * n_col // count
        n_src = sources.shape[0]
        table = cas_matrix(extent)
        kernel = kernel_grid(extent)
        cos_h, sin_h, live = shift_tables(column_length, depth, extent)
        slot = jnp.arange(depth, dtype=jnp.int32)
        fwd = jnp.concatenate([table[:depth], table[(extent - slot) % extent]], axis=1)
        bwd = jnp.concatenate([table[:, :depth], table[:, (extent - slot) % extent]], axis=0)
        w = lax.optimization_barrier(plane_matrix(column_cell, table, extent))

        own_blocks = exchange(orbitals, "col", n_col)
        g = lax.axis_index("grp")
        owner = sources // n_grp_bands
        picked = orbitals[sources % n_grp_bands]
        picked = jnp.where((owner == g)[:, None], picked, 0.0)
        spread = jnp.broadcast_to(picked[None], (n_grp, n_src, width))
        picked = jnp.sum(exchange(spread, "grp", n_grp), axis=0)
        src_blocks = exchange(jnp.broadcast_to(picked[None], (n_col, n_src, width)), "col", n_col)
        got = jnp.concatenate([own_blocks[:, None, :], src_blocks], axis=1)
        n = 1 + n_src
        coeff = got.reshape(n_col, n, width // depth, depth).transpose(0, 2, 1, 3).reshape(count, n, depth)
        coeff = jnp.where(live[:, None, :], coeff, 0.0)
        both = jnp.dot(coeff.reshape(count * n, depth), fwd, precision=MID).reshape(count, n, 2, extent)
        cols = cos_h[:, None, :] * both[:, :, 0] - sin_h[:, None, :] * both[:, :, 1]
        grids = jnp.dot(w, cols.reshape(count, n * extent), precision=MID)
        grids = grids.reshape(extent, extent, n, extent)
        own = grids[:, :, :1]
        src = grids[:, :, 1:]
        density = own * src
        potential = cas_three(kernel[:, :, None, :] * cas_three(density, table), table)
        total = jnp.sum(weights[None, None, :, None] * potential * src, axis=2)
        back = lax.dot_general(w, total.reshape(extent * extent, extent), (((0,), (0,)), ((), ())), precision=MID)
        scaled = jnp.concatenate([back * cos_h, -(back * sin_h)], axis=1)
        out = -jnp.dot(scaled, bwd, precision=MID)
        out = jnp.where(live, out, 0.0)
        return exchange(out.reshape(n_col, width), "col", n_col)

    return local


def solution(mesh):
    n_grp = mesh.shape["grp"]
    n_col = mesh.shape["col"]

    def run(orbitals, column_cell, column_length, sources, weights):
        n_grp_bands = orbitals.shape[0] // n_grp
        body = make_local(n_grp_bands, n_grp, n_col)
        return jax.shard_map(
            body,
            mesh=mesh,
            in_specs=(P("grp", "col"), P(), P(), P(), P()),
            out_specs=P("grp", "col"),
            check_vma=False,
        )(orbitals, column_cell, column_length, sources, weights)

    return run
```

```python
import math

import jax
import jax.numpy as jnp
from jax import lax
from jax.sharding import PartitionSpec as P

GRID = 48

kernel_scale = 20000.0
screen_shift = 4.0

HI = lax.Precision.HIGHEST
MID = lax.Precision.HIGH


def cas_matrix(extent):
    index = jnp.arange(extent, dtype=jnp.int32)
    phase = index[:, None] * index[None, :] % extent
    angle = phase.astype(jnp.float32) * (2.0 * math.pi / extent)
    return (jnp.cos(angle) + jnp.sin(angle)) / math.sqrt(extent)


def kernel_grid(extent):
    index = jnp.arange(extent, dtype=jnp.int32)
    freq = jnp.minimum(index, extent - index)
    square = freq * freq
    total = square[:, None, None] + square[None, :, None] + square[None, None, :]
    kernel = kernel_scale / (total.astype(jnp.float32) + screen_shift)
    return jnp.where(total > 0, kernel, 0.0)


def shift_tables(column_length, depth, extent):
    half = column_length // 2
    index = jnp.arange(extent, dtype=jnp.int32)
    phase = (half[:, None] * index[None, :]) % extent
    angle = phase.astype(jnp.float32) * (2.0 * math.pi / extent)
    slot = jnp.arange(depth, dtype=jnp.int32)
    live = slot[None, :] < column_length[:, None]
    return jnp.cos(angle), jnp.sin(angle), live


def plane_matrix(column_cell, table, extent):
    index = jnp.arange(extent, dtype=jnp.int32)
    first = (column_cell[None, :] // extent == index[:, None]).astype(jnp.float32)
    second = (column_cell[None, :] % extent == index[:, None]).astype(jnp.float32)
    ta = jnp.dot(table, first, precision=HI)
    tb = jnp.dot(table, second, precision=HI)
    return (ta[:, None, :] * tb[None, :, :]).reshape(extent * extent, -1)


def along_last(field, table):
    shape = field.shape
    return jnp.dot(field.reshape(-1, shape[-1]), table, precision=MID).reshape(shape)


def along_first(field, table):
    shape = field.shape
    return jnp.dot(table, field.reshape(shape[0], -1), precision=MID).reshape(shape)


def swap(field):
    return jnp.swapaxes(field, 0, 1)


def make_local(n_grp_bands, n_grp, n_col):
    def local(orbitals, column_cell, column_length, sources, weights):
        extent = GRID
        count = column_cell.shape[0]
        width = orbitals.shape[1]
        depth = width * n_col // count
        n_src = sources.shape[0]
        table = cas_matrix(extent)
        kernel = kernel_grid(extent)
        cos_h, sin_h, live = shift_tables(column_length, depth, extent)
        slot = jnp.arange(depth, dtype=jnp.int32)
        fwd = jnp.concatenate([table[:depth], table[(extent - slot) % extent]], axis=1)
        bwd = jnp.concatenate([table[:, :depth], table[:, (extent - slot) % extent]], axis=0)
        w = lax.optimization_barrier(plane_matrix(column_cell, table, extent))

        g = lax.axis_index("grp")
        owner = sources // n_grp_bands
        picked = orbitals[sources % n_grp_bands]
        picked = jnp.where((owner == g)[:, None], picked, 0.0)
        spread = jnp.broadcast_to(picked[None], (n_grp, n_src, width))
        picked = jnp.sum(lax.all_to_all(spread, "grp", 0, 0, tiled=True), axis=0)
        send = jnp.concatenate(
            [orbitals[:, None, :], jnp.broadcast_to(picked[None], (n_grp_bands, n_src, width))], axis=1)
        got = lax.all_to_all(send, "col", 0, 0, tiled=True)
        n = 1 + n_src
        coeff = got.reshape(n_col, n, width // depth, depth).transpose(0, 2, 1, 3).reshape(count, n, depth)
        coeff = jnp.where(live[:, None, :], coeff, 0.0)
        both = jnp.dot(coeff.reshape(count * n, depth), fwd, precision=MID).reshape(count, n, 2, extent)
        cols = cos_h[:, None, :] * both[:, :, 0] - sin_h[:, None, :] * both[:, :, 1]
        grids = jnp.dot(w, cols.reshape(count, n * extent), precision=MID)
        grids = grids.reshape(extent, extent, n, extent)
        own = grids[:, :, :1]
        src = grids[:, :, 1:]
        density = own * src
        field = along_first(along_last(density, table), table)
        field = along_first(swap(field), table)
        field = kernel[:, :, None, :] * field
        field = along_first(along_last(field, table), table)
        potential = along_first(swap(field), table)
        total = jnp.sum(weights[None, None, :, None] * potential * src, axis=2)
        back = lax.dot_general(w, total.reshape(extent * extent, extent), (((0,), (0,)), ((), ())), precision=MID)
        scaled = jnp.concatenate([back * cos_h, -(back * sin_h)], axis=1)
        out = -jnp.dot(scaled, bwd, precision=MID)
        out = jnp.where(live, out, 0.0)
        return lax.all_to_all(out.reshape(n_col, 1, width), "col", 0, 0, tiled=True).reshape(n_col, width)

    return local


def solution(mesh):
    n_grp = mesh.shape["grp"]
    n_col = mesh.shape["col"]

    def run(orbitals, column_cell, column_length, sources, weights):
        n_grp_bands = orbitals.shape[0] // n_grp
        body = make_local(n_grp_bands, n_grp, n_col)
        return jax.shard_map(
            body,
            mesh=mesh,
            in_specs=(P("grp", "col"), P(), P(), P(), P()),
            out_specs=P("grp", "col"),
            check_vma=False,
        )(orbitals, column_cell, column_length, sources, weights)

    return run
```

```python
import math

import jax
import jax.numpy as jnp
from jax import lax
from jax.sharding import PartitionSpec as P

GRID = 48

kernel_scale = 20000.0
screen_shift = 4.0

HI = lax.Precision.HIGHEST
MID = lax.Precision.HIGH


def cas_matrix(extent):
    index = jnp.arange(extent, dtype=jnp.int32)
    phase = index[:, None] * index[None, :] % extent
    angle = phase.astype(jnp.float32) * (2.0 * math.pi / extent)
    return (jnp.cos(angle) + jnp.sin(angle)) / math.sqrt(extent)


def kernel_grid(extent):
    index = jnp.arange(extent, dtype=jnp.int32)
    freq = jnp.minimum(index, extent - index)
    square = freq * freq
    total = square[:, None, None] + square[None, :, None] + square[None, None, :]
    kernel = kernel_scale / (total.astype(jnp.float32) + screen_shift)
    return jnp.where(total > 0, kernel, 0.0)


def shift_tables(column_length, depth, extent):
    half = column_length // 2
    index = jnp.arange(extent, dtype=jnp.int32)
    phase = (half[:, None] * index[None, :]) % extent
    angle = phase.astype(jnp.float32) * (2.0 * math.pi / extent)
    slot = jnp.arange(depth, dtype=jnp.int32)
    live = slot[None, :] < column_length[:, None]
    return jnp.cos(angle), jnp.sin(angle), live


def plane_matrix(column_cell, table, extent):
    index = jnp.arange(extent, dtype=jnp.int32)
    first = (column_cell[None, :] // extent == index[:, None]).astype(jnp.float32)
    second = (column_cell[None, :] % extent == index[:, None]).astype(jnp.float32)
    ta = jnp.dot(table, first, precision=HI)
    tb = jnp.dot(table, second, precision=HI)
    return (ta[:, None, :] * tb[None, :, :]).reshape(extent * extent, -1)


def cas_three(field, table):
    field = jnp.einsum("absc,ck->absk", field, table, precision=MID)
    field = jnp.einsum("absc,kb->aksc", field, table, precision=MID)
    return jnp.einsum("absc,ka->kbsc", field, table, precision=MID)


def make_local(n_grp_bands, n_grp, n_col):
    def local(orbitals, column_cell, column_length, sources, weights):
        extent = GRID
        count = column_cell.shape[0]
        width = orbitals.shape[1]
        depth = width * n_col // count
        n_src = sources.shape[0]

        g = lax.axis_index("grp")
        owner = sources // n_grp_bands
        rows = (sources % n_grp_bands)[:, None] == jnp.arange(n_grp_bands, dtype=jnp.int32)[None, :]
        picked = jnp.dot(rows.astype(jnp.float32), orbitals, precision=HI)
        picked = jnp.where((owner == g)[:, None], picked, 0.0)
        spread = jnp.broadcast_to(picked[None], (n_grp, n_src, width))
        picked = jnp.sum(lax.all_to_all(spread, "grp", 0, 0, tiled=True), axis=0)
        send = jnp.concatenate(
            [orbitals[:, None, :], jnp.broadcast_to(picked[None], (n_grp_bands, n_src, width))], axis=1)
        send, column_cell, column_length = lax.optimization_barrier((send, column_cell, column_length))
        got = lax.all_to_all(send, "col", 0, 0, tiled=True)
        table = cas_matrix(extent) + 0.0 * column_length[0]
        kernel = kernel_grid(extent)
        cos_h, sin_h, live = shift_tables(column_length, depth, extent)
        slot = jnp.arange(depth, dtype=jnp.int32)
        fwd = jnp.concatenate([table[:depth], table[(extent - slot) % extent]], axis=1)
        bwd = jnp.concatenate([table[:, :depth], table[:, (extent - slot) % extent]], axis=0)
        w = lax.optimization_barrier(plane_matrix(column_cell, table, extent))
        n = 1 + n_src
        coeff = got.reshape(n_col, n, width // depth, depth).transpose(0, 2, 1, 3).reshape(count, n, depth)
        coeff = jnp.where(live[:, None, :], coeff, 0.0)
        both = jnp.dot(coeff.reshape(count * n, depth), fwd, precision=MID).reshape(count, n, 2, extent)
        cols = cos_h[:, None, :] * both[:, :, 0] - sin_h[:, None, :] * both[:, :, 1]
        grids = jnp.dot(w, cols.reshape(count, n * extent), precision=MID)
        grids = grids.reshape(extent, extent, n, extent)
        own = grids[:, :, :1]
        src = grids[:, :, 1:]
        density = own * src
        potential = cas_three(kernel[:, :, None, :] * cas_three(density, table), table)
        total = jnp.sum(weights[None, None, :, None] * potential * src, axis=2)
        back = lax.dot_general(w, total.reshape(extent * extent, extent), (((0,), (0,)), ((), ())), precision=MID)
        scaled = jnp.concatenate([back * cos_h, -(back * sin_h)], axis=1)
        out = -jnp.dot(scaled, bwd, precision=MID)
        out = jnp.where(live, out, 0.0)
        return lax.all_to_all(out.reshape(n_col, 1, width), "col", 0, 0, tiled=True).reshape(n_col, width)

    return local


def solution(mesh):
    n_grp = mesh.shape["grp"]
    n_col = mesh.shape["col"]

    def run(orbitals, column_cell, column_length, sources, weights):
        n_grp_bands = orbitals.shape[0] // n_grp
        body = make_local(n_grp_bands, n_grp, n_col)
        return jax.shard_map(
            body,
            mesh=mesh,
            in_specs=(P("grp", "col"), P(), P(), P(), P()),
            out_specs=P("grp", "col"),
            check_vma=False,
        )(orbitals, column_cell, column_length, sources, weights)

    return run
```

```python
import math

import jax
import jax.numpy as jnp
from jax import lax
from jax.sharding import PartitionSpec as P

GRID = 48

kernel_scale = 20000.0
screen_shift = 4.0

HI = lax.Precision.HIGHEST
MID = lax.Precision.HIGH


def cas_matrix(extent):
    index = jnp.arange(extent, dtype=jnp.int32)
    phase = index[:, None] * index[None, :] % extent
    angle = phase.astype(jnp.float32) * (2.0 * math.pi / extent)
    return (jnp.cos(angle) + jnp.sin(angle)) / math.sqrt(extent)


def kernel_grid(extent):
    index = jnp.arange(extent, dtype=jnp.int32)
    freq = jnp.minimum(index, extent - index)
    square = freq * freq
    total = square[:, None, None] + square[None, :, None] + square[None, None, :]
    kernel = kernel_scale / (total.astype(jnp.float32) + screen_shift)
    return jnp.where(total > 0, kernel, 0.0)


def shift_tables(column_length, depth, extent):
    half = column_length // 2
    index = jnp.arange(extent, dtype=jnp.int32)
    phase = (half[:, None] * index[None, :]) % extent
    angle = phase.astype(jnp.float32) * (2.0 * math.pi / extent)
    slot = jnp.arange(depth, dtype=jnp.int32)
    live = slot[None, :] < column_length[:, None]
    return jnp.cos(angle), jnp.sin(angle), live


def plane_matrix(column_cell, table, extent):
    index = jnp.arange(extent, dtype=jnp.int32)
    first = (column_cell[None, :] // extent == index[:, None]).astype(jnp.float32)
    second = (column_cell[None, :] % extent == index[:, None]).astype(jnp.float32)
    ta = jnp.dot(table, first, precision=HI)
    tb = jnp.dot(table, second, precision=HI)
    return (ta[:, None, :] * tb[None, :, :]).reshape(extent * extent, -1)


def cas_three(field, table):
    field = jnp.einsum("absc,ck->absk", field, table, precision=MID)
    field = jnp.einsum("absc,kb->aksc", field, table, precision=MID)
    return jnp.einsum("absc,ka->kbsc", field, table, precision=MID)


def make_local(n_grp_bands, n_grp, n_col):
    def local(orbitals, column_cell, column_length, sources, weights):
        extent = GRID
        count = column_cell.shape[0]
        width = orbitals.shape[1]
        depth = width * n_col // count
        n_src = sources.shape[0]

        g = lax.axis_index("grp")
        owner = sources // n_grp_bands
        rows = (sources % n_grp_bands)[:, None] == jnp.arange(n_grp_bands, dtype=jnp.int32)[None, :]
        picked = jnp.dot(rows.astype(jnp.float32), orbitals, precision=HI)
        picked = jnp.where((owner == g)[:, None], picked, 0.0)
        spread = jnp.broadcast_to(picked[None], (n_grp, n_src, width))
        spread = spread.reshape(n_grp, n_src * width // 128, 128)
        picked = jnp.sum(lax.all_to_all(spread, "grp", 0, 0, tiled=True), axis=0).reshape(n_src, width)
        send = jnp.concatenate(
            [orbitals[:, None, :], jnp.broadcast_to(picked[None], (n_grp_bands, n_src, width))], axis=1)
        send, column_cell, column_length = lax.optimization_barrier((send, column_cell, column_length))
        got = lax.all_to_all(send.reshape(n_grp_bands, -1, 128), "col", 0, 0, tiled=True)
        got = got.reshape(n_col, 1 + n_src, width)
        table = cas_matrix(extent) + 0.0 * column_length[0]
        kernel = kernel_grid(extent)
        cos_h, sin_h, live = shift_tables(column_length, depth, extent)
        slot = jnp.arange(depth, dtype=jnp.int32)
        fwd = jnp.concatenate([table[:depth], table[(extent - slot) % extent]], axis=1)
        bwd = jnp.concatenate([table[:, :depth], table[:, (extent - slot) % extent]], axis=0)
        w = lax.optimization_barrier(plane_matrix(column_cell, table, extent))
        n = 1 + n_src
        coeff = got.reshape(n_col, n, width // depth, depth).transpose(0, 2, 1, 3).reshape(count, n, depth)
        coeff = jnp.where(live[:, None, :], coeff, 0.0)
        both = jnp.dot(coeff.reshape(count * n, depth), fwd, precision=MID).reshape(count, n, 2, extent)
        cols = cos_h[:, None, :] * both[:, :, 0] - sin_h[:, None, :] * both[:, :, 1]
        grids = jnp.dot(w, cols.reshape(count, n * extent), precision=MID)
        grids = grids.reshape(extent, extent, n, extent)
        own = grids[:, :, :1]
        src = grids[:, :, 1:]
        density = own * src
        potential = cas_three(kernel[:, :, None, :] * cas_three(density, table), table)
        total = jnp.sum(weights[None, None, :, None] * potential * src, axis=2)
        back = lax.dot_general(w, total.reshape(extent * extent, extent), (((0,), (0,)), ((), ())), precision=MID)
        scaled = jnp.concatenate([back * cos_h, -(back * sin_h)], axis=1)
        out = -jnp.dot(scaled, bwd, precision=MID)
        out = jnp.where(live, out, 0.0)
        back = lax.all_to_all(out.reshape(n_col, width // 128, 128), "col", 0, 0, tiled=True)
        return back.reshape(n_col, width)

    return local


def solution(mesh):
    n_grp = mesh.shape["grp"]
    n_col = mesh.shape["col"]

    def run(orbitals, column_cell, column_length, sources, weights):
        n_grp_bands = orbitals.shape[0] // n_grp
        body = make_local(n_grp_bands, n_grp, n_col)
        return jax.shard_map(
            body,
            mesh=mesh,
            in_specs=(P("grp", "col"), P(), P(), P(), P()),
            out_specs=P("grp", "col"),
            check_vma=False,
        )(orbitals, column_cell, column_length, sources, weights)

    return run
```

```python
import math

import jax
import jax.numpy as jnp
from jax import lax
from jax.sharding import PartitionSpec as P

GRID = 48

kernel_scale = 20000.0
screen_shift = 4.0

HI = lax.Precision.HIGHEST
MID = lax.Precision.HIGH


def cas_matrix(extent):
    index = jnp.arange(extent, dtype=jnp.int32)
    phase = index[:, None] * index[None, :] % extent
    angle = phase.astype(jnp.float32) * (2.0 * math.pi / extent)
    return (jnp.cos(angle) + jnp.sin(angle)) / math.sqrt(extent)


def kernel_grid(extent):
    index = jnp.arange(extent, dtype=jnp.int32)
    freq = jnp.minimum(index, extent - index)
    square = freq * freq
    total = square[:, None, None] + square[None, :, None] + square[None, None, :]
    kernel = kernel_scale / (total.astype(jnp.float32) + screen_shift)
    return jnp.where(total > 0, kernel, 0.0)


def shift_tables(column_length, depth, extent):
    half = column_length // 2
    index = jnp.arange(extent, dtype=jnp.int32)
    phase = (half[:, None] * index[None, :]) % extent
    angle = phase.astype(jnp.float32) * (2.0 * math.pi / extent)
    slot = jnp.arange(depth, dtype=jnp.int32)
    live = slot[None, :] < column_length[:, None]
    return jnp.cos(angle), jnp.sin(angle), live


def plane_matrix(column_cell, table, extent):
    index = jnp.arange(extent, dtype=jnp.int32)
    first = (column_cell[None, :] // extent == index[:, None]).astype(jnp.float32)
    second = (column_cell[None, :] % extent == index[:, None]).astype(jnp.float32)
    ta = jnp.dot(table, first, precision=HI)
    tb = jnp.dot(table, second, precision=HI)
    return (ta[:, None, :] * tb[None, :, :]).reshape(extent * extent, -1)


def halves(value):
    high = lax.reduce_precision(value, exponent_bits=8, mantissa_bits=7)
    return high.astype(jnp.bfloat16), (value - high).astype(jnp.bfloat16)


def stacked(table):
    high, low = halves(table)
    return jnp.concatenate([high, low, high], axis=0)


def split_stack(field, axis):
    high, low = halves(field)
    return jnp.concatenate([high, high, low], axis=axis)


def cas_three(field, table):
    parts = stacked(table)
    field = jnp.einsum("absc,ck->absk", split_stack(field, 3), parts, preferred_element_type=jnp.float32)
    field = jnp.einsum("absc,kb->aksc", split_stack(field, 1), parts.T, preferred_element_type=jnp.float32)
    return jnp.einsum("absc,ka->kbsc", split_stack(field, 0), parts.T, preferred_element_type=jnp.float32)


def make_local(n_grp_bands, n_grp, n_col):
    def local(orbitals, column_cell, column_length, sources, weights):
        extent = GRID
        count = column_cell.shape[0]
        width = orbitals.shape[1]
        depth = width * n_col // count
        n_src = sources.shape[0]

        g = lax.axis_index("grp")
        owner = sources // n_grp_bands
        rows = (sources % n_grp_bands)[:, None] == jnp.arange(n_grp_bands, dtype=jnp.int32)[None, :]
        picked = jnp.dot(rows.astype(jnp.float32), orbitals, precision=HI)
        picked = jnp.where((owner == g)[:, None], picked, 0.0)
        spread = jnp.broadcast_to(picked[None], (n_grp, n_src, width))
        picked = jnp.sum(lax.all_to_all(spread, "grp", 0, 0, tiled=True), axis=0)
        send = jnp.concatenate(
            [orbitals[:, None, :], jnp.broadcast_to(picked[None], (n_grp_bands, n_src, width))], axis=1)
        send, column_cell, column_length = lax.optimization_barrier((send, column_cell, column_length))
        got = lax.all_to_all(send, "col", 0, 0, tiled=True)
        table = cas_matrix(extent) + 0.0 * column_length[0]
        kernel = kernel_grid(extent)
        cos_h, sin_h, live = shift_tables(column_length, depth, extent)
        slot = jnp.arange(depth, dtype=jnp.int32)
        fwd = jnp.concatenate([table[:depth], table[(extent - slot) % extent]], axis=1)
        bwd = jnp.concatenate([table[:, :depth], table[:, (extent - slot) % extent]], axis=0)
        w = lax.optimization_barrier(plane_matrix(column_cell, table, extent))
        n = 1 + n_src
        coeff = got.reshape(n_col, n, width // depth, depth).transpose(0, 2, 1, 3).reshape(count, n, depth)
        coeff = jnp.where(live[:, None, :], coeff, 0.0)
        both = jnp.dot(coeff.reshape(count * n, depth), fwd, precision=MID).reshape(count, n, 2, extent)
        cols = cos_h[:, None, :] * both[:, :, 0] - sin_h[:, None, :] * both[:, :, 1]
        grids = jnp.dot(w, cols.reshape(count, n * extent), precision=MID)
        grids = grids.reshape(extent, extent, n, extent)
        own = grids[:, :, :1]
        src = grids[:, :, 1:]
        density = own * src
        potential = cas_three(kernel[:, :, None, :] * cas_three(density, table), table)
        total = jnp.sum(weights[None, None, :, None] * potential * src, axis=2)
        back = lax.dot_general(w, total.reshape(extent * extent, extent), (((0,), (0,)), ((), ())), precision=MID)
        scaled = jnp.concatenate([back * cos_h, -(back * sin_h)], axis=1)
        out = -jnp.dot(scaled, bwd, precision=MID)
        out = jnp.where(live, out, 0.0)
        return lax.all_to_all(out.reshape(n_col, 1, width), "col", 0, 0, tiled=True).reshape(n_col, width)

    return local


def solution(mesh):
    n_grp = mesh.shape["grp"]
    n_col = mesh.shape["col"]

    def run(orbitals, column_cell, column_length, sources, weights):
        n_grp_bands = orbitals.shape[0] // n_grp
        body = make_local(n_grp_bands, n_grp, n_col)
        return jax.shard_map(
            body,
            mesh=mesh,
            in_specs=(P("grp", "col"), P(), P(), P(), P()),
            out_specs=P("grp", "col"),
            check_vma=False,
        )(orbitals, column_cell, column_length, sources, weights)

    return run
```

```python
import math

import jax
import jax.numpy as jnp
from jax import lax
from jax.sharding import PartitionSpec as P

GRID = 48

kernel_scale = 20000.0
screen_shift = 4.0

HI = lax.Precision.HIGHEST
MID = lax.Precision.HIGH


def cas_matrix(extent):
    index = jnp.arange(extent, dtype=jnp.int32)
    phase = index[:, None] * index[None, :] % extent
    angle = phase.astype(jnp.float32) * (2.0 * math.pi / extent)
    return (jnp.cos(angle) + jnp.sin(angle)) / math.sqrt(extent)


def kernel_grid(extent):
    index = jnp.arange(extent, dtype=jnp.int32)
    freq = jnp.minimum(index, extent - index)
    square = freq * freq
    total = square[:, None, None] + square[None, :, None] + square[None, None, :]
    kernel = kernel_scale / (total.astype(jnp.float32) + screen_shift)
    return jnp.where(total > 0, kernel, 0.0)


def shift_tables(column_length, depth, extent):
    half = column_length // 2
    index = jnp.arange(extent, dtype=jnp.int32)
    phase = (half[:, None] * index[None, :]) % extent
    angle = phase.astype(jnp.float32) * (2.0 * math.pi / extent)
    slot = jnp.arange(depth, dtype=jnp.int32)
    live = slot[None, :] < column_length[:, None]
    return jnp.cos(angle), jnp.sin(angle), live


def plane_matrix(column_cell, table, extent):
    index = jnp.arange(extent, dtype=jnp.int32)
    first = (column_cell[None, :] // extent == index[:, None]).astype(jnp.float32)
    second = (column_cell[None, :] % extent == index[:, None]).astype(jnp.float32)
    ta = jnp.dot(table, first, precision=HI)
    tb = jnp.dot(table, second, precision=HI)
    return (ta[:, None, :] * tb[None, :, :]).reshape(extent * extent, -1)


def cas_three(field, table):
    field = jnp.einsum("absc,ck->absk", field, table, precision=MID)
    field = jnp.einsum("absc,kb->aksc", field, table, precision=MID)
    return jnp.einsum("absc,ka->kbsc", field, table, precision=MID)


def make_local(n_grp_bands, n_grp, n_col):
    def local(orbitals, column_cell, column_length, sources, weights):
        extent = GRID
        count = column_cell.shape[0]
        width = orbitals.shape[1]
        depth = width * n_col // count
        n_src = sources.shape[0]

        g = lax.axis_index("grp")
        owner = sources // n_grp_bands
        rows = (sources % n_grp_bands)[:, None] == jnp.arange(n_grp_bands, dtype=jnp.int32)[None, :]
        picked = jnp.dot(rows.astype(jnp.float32), orbitals, precision=HI)
        picked = jnp.where((owner == g)[:, None], picked, 0.0)
        send = jnp.concatenate(
            [orbitals[:, None, :], jnp.broadcast_to(picked[None], (n_grp_bands, n_src, width))], axis=1)
        send = jnp.broadcast_to(send[None], (n_grp,) + send.shape).reshape((n_grp * n_col,) + send.shape[1:])
        send, column_cell, column_length = lax.optimization_barrier((send, column_cell, column_length))
        got = lax.all_to_all(send, ("grp", "col"), 0, 0, tiled=True)
        got = got.reshape(n_grp, n_col, 1 + n_src, width)
        own_blocks = lax.dynamic_index_in_dim(got[:, :, 0], g, 0, keepdims=False)
        got = jnp.concatenate([own_blocks[:, None, :], jnp.sum(got[:, :, 1:], axis=0)], axis=1)
        table = cas_matrix(extent) + 0.0 * column_length[0]
        kernel = kernel_grid(extent)
        cos_h, sin_h, live = shift_tables(column_length, depth, extent)
        slot = jnp.arange(depth, dtype=jnp.int32)
        fwd = jnp.concatenate([table[:depth], table[(extent - slot) % extent]], axis=1)
        bwd = jnp.concatenate([table[:, :depth], table[:, (extent - slot) % extent]], axis=0)
        w = lax.optimization_barrier(plane_matrix(column_cell, table, extent))
        n = 1 + n_src
        coeff = got.reshape(n_col, n, width // depth, depth).transpose(0, 2, 1, 3).reshape(count, n, depth)
        coeff = jnp.where(live[:, None, :], coeff, 0.0)
        both = jnp.dot(coeff.reshape(count * n, depth), fwd, precision=MID).reshape(count, n, 2, extent)
        cols = cos_h[:, None, :] * both[:, :, 0] - sin_h[:, None, :] * both[:, :, 1]
        grids = jnp.dot(w, cols.reshape(count, n * extent), precision=MID)
        grids = grids.reshape(extent, extent, n, extent)
        own = grids[:, :, :1]
        src = grids[:, :, 1:]
        density = own * src
        potential = cas_three(kernel[:, :, None, :] * cas_three(density, table), table)
        total = jnp.sum(weights[None, None, :, None] * potential * src, axis=2)
        back = lax.dot_general(w, total.reshape(extent * extent, extent), (((0,), (0,)), ((), ())), precision=MID)
        scaled = jnp.concatenate([back * cos_h, -(back * sin_h)], axis=1)
        out = -jnp.dot(scaled, bwd, precision=MID)
        out = jnp.where(live, out, 0.0)
        return lax.all_to_all(out.reshape(n_col, 1, width), "col", 0, 0, tiled=True).reshape(n_col, width)

    return local


def solution(mesh):
    n_grp = mesh.shape["grp"]
    n_col = mesh.shape["col"]

    def run(orbitals, column_cell, column_length, sources, weights):
        n_grp_bands = orbitals.shape[0] // n_grp
        body = make_local(n_grp_bands, n_grp, n_col)
        return jax.shard_map(
            body,
            mesh=mesh,
            in_specs=(P("grp", "col"), P(), P(), P(), P()),
            out_specs=P("grp", "col"),
            check_vma=False,
        )(orbitals, column_cell, column_length, sources, weights)

    return run
```

```python
import math

import jax
import jax.numpy as jnp
from jax import lax
from jax.sharding import PartitionSpec as P

GRID = 48

kernel_scale = 20000.0
screen_shift = 4.0

HI = lax.Precision.HIGHEST
MID = lax.Precision.HIGH


def cas_matrix(extent):
    index = jnp.arange(extent, dtype=jnp.int32)
    phase = index[:, None] * index[None, :] % extent
    angle = phase.astype(jnp.float32) * (2.0 * math.pi / extent)
    return (jnp.cos(angle) + jnp.sin(angle)) / math.sqrt(extent)


def kernel_grid(extent):
    index = jnp.arange(extent, dtype=jnp.int32)
    freq = jnp.minimum(index, extent - index)
    square = freq * freq
    total = square[:, None, None] + square[None, :, None] + square[None, None, :]
    kernel = kernel_scale / (total.astype(jnp.float32) + screen_shift)
    return jnp.where(total > 0, kernel, 0.0)


def shift_tables(column_length, depth, extent):
    half = column_length // 2
    index = jnp.arange(extent, dtype=jnp.int32)
    phase = (half[:, None] * index[None, :]) % extent
    angle = phase.astype(jnp.float32) * (2.0 * math.pi / extent)
    slot = jnp.arange(depth, dtype=jnp.int32)
    live = slot[None, :] < column_length[:, None]
    return jnp.cos(angle), jnp.sin(angle), live


def plane_matrix(column_cell, table, extent):
    index = jnp.arange(extent, dtype=jnp.int32)
    first = (column_cell[None, :] // extent == index[:, None]).astype(jnp.float32)
    second = (column_cell[None, :] % extent == index[:, None]).astype(jnp.float32)
    ta = jnp.dot(table, first, precision=HI)
    tb = jnp.dot(table, second, precision=HI)
    return (ta[:, None, :] * tb[None, :, :]).reshape(extent * extent, -1)


def cas_three(field, table):
    field = jnp.einsum("absc,ck->absk", field, table, precision=MID)
    field = jnp.einsum("absc,kb->aksc", field, table, precision=MID)
    return jnp.einsum("absc,ka->kbsc", field, table, precision=MID)


def make_local(n_grp_bands, n_grp, n_col):
    def local(orbitals, column_cell, column_length, sources, weights):
        extent = GRID
        count = column_cell.shape[0]
        width = orbitals.shape[1]
        depth = width * n_col // count
        n_src = sources.shape[0]

        g = lax.axis_index("grp")
        owner = sources // n_grp_bands
        rows = (sources % n_grp_bands)[:, None] == jnp.arange(n_grp_bands, dtype=jnp.int32)[None, :]
        picked = jnp.dot(rows.astype(jnp.float32), orbitals, precision=HI)
        picked = jnp.where((owner == g)[:, None], picked, 0.0)
        spread = jnp.broadcast_to(picked[None], (n_grp, n_src, width))
        picked = jnp.sum(lax.all_to_all(spread, "grp", 0, 0, tiled=True), axis=0)
        send = jnp.concatenate(
            [orbitals[:, None, :], jnp.broadcast_to(picked[None], (n_grp_bands, n_src, width))], axis=1)
        send, column_cell, column_length = lax.optimization_barrier((send, column_cell, column_length))
        got = lax.all_to_all(send, "col", 0, 0, tiled=True)
        table = cas_matrix(extent) + 0.0 * column_length[0]
        kernel = kernel_grid(extent)
        cos_h, sin_h, live = shift_tables(column_length, depth, extent)
        slot = jnp.arange(depth, dtype=jnp.int32)
        fwd = jnp.concatenate([table[:depth], table[(extent - slot) % extent]], axis=1)
        bwd = jnp.concatenate([table[:, :depth], table[:, (extent - slot) % extent]], axis=0)
        w = lax.optimization_barrier(plane_matrix(column_cell, table, extent))
        n = 1 + n_src
        coeff = got.reshape(n_col, n, width // depth, depth).transpose(0, 2, 1, 3).reshape(count, n, depth)
        coeff = jnp.where(live[:, None, :], coeff, 0.0)
        both = jnp.dot(coeff.reshape(count * n, depth), fwd, precision=MID).reshape(count, n, 2, extent)
        cols = cos_h[:, None, :] * both[:, :, 0] - sin_h[:, None, :] * both[:, :, 1]
        grids = jnp.dot(w, cols.reshape(count, n * extent), precision=MID)
        grids = grids.reshape(extent, extent, n, extent)
        own = grids[:, :, :1]
        src = grids[:, :, 1:]
        density = own * src
        field = jnp.einsum("absc,ck->absk", density, table, precision=MID)
        field = jnp.einsum("absk,lb->askl", field, table, precision=MID)
        field = jnp.einsum("askl,ma->sklm", field, table, precision=MID)
        field = kernel[None] * field
        field = jnp.einsum("sxyz,zw->sxyw", field, table, precision=MID)
        field = jnp.einsum("sxyw,vy->sxwv", field, table, precision=MID)
        potential = jnp.einsum("sxwv,ux->swvu", field, table, precision=MID)
        total = jnp.sum(weights[:, None, None, None] * potential * jnp.transpose(src, (2, 0, 1, 3)), axis=0)
        back = lax.dot_general(w, total.reshape(extent * extent, extent), (((0,), (0,)), ((), ())), precision=MID)
        scaled = jnp.concatenate([back * cos_h, -(back * sin_h)], axis=1)
        out = -jnp.dot(scaled, bwd, precision=MID)
        out = jnp.where(live, out, 0.0)
        return lax.all_to_all(out.reshape(n_col, 1, width), "col", 0, 0, tiled=True).reshape(n_col, width)

    return local


def solution(mesh):
    n_grp = mesh.shape["grp"]
    n_col = mesh.shape["col"]

    def run(orbitals, column_cell, column_length, sources, weights):
        n_grp_bands = orbitals.shape[0] // n_grp
        body = make_local(n_grp_bands, n_grp, n_col)
        return jax.shard_map(
            body,
            mesh=mesh,
            in_specs=(P("grp", "col"), P(), P(), P(), P()),
            out_specs=P("grp", "col"),
            check_vma=False,
        )(orbitals, column_cell, column_length, sources, weights)

    return run
```

```python
import math

import jax
import jax.numpy as jnp
from jax import lax
from jax.sharding import PartitionSpec as P

GRID = 48

kernel_scale = 20000.0
screen_shift = 4.0

HI = lax.Precision.HIGHEST
MID = lax.Precision.HIGH


def cas_matrix(extent):
    index = jnp.arange(extent, dtype=jnp.int32)
    phase = index[:, None] * index[None, :] % extent
    angle = phase.astype(jnp.float32) * (2.0 * math.pi / extent)
    return (jnp.cos(angle) + jnp.sin(angle)) / math.sqrt(extent)


def kernel_grid(extent):
    index = jnp.arange(extent, dtype=jnp.int32)
    freq = jnp.minimum(index, extent - index)
    square = freq * freq
    total = square[:, None, None] + square[None, :, None] + square[None, None, :]
    kernel = kernel_scale / (total.astype(jnp.float32) + screen_shift)
    return jnp.where(total > 0, kernel, 0.0)


def shift_tables(column_length, depth, extent):
    half = column_length // 2
    index = jnp.arange(extent, dtype=jnp.int32)
    phase = (half[:, None] * index[None, :]) % extent
    angle = phase.astype(jnp.float32) * (2.0 * math.pi / extent)
    slot = jnp.arange(depth, dtype=jnp.int32)
    live = slot[None, :] < column_length[:, None]
    return jnp.cos(angle), jnp.sin(angle), live


def plane_matrix(column_cell, table, extent):
    index = jnp.arange(extent, dtype=jnp.int32)
    first = (column_cell[None, :] // extent == index[:, None]).astype(jnp.float32)
    second = (column_cell[None, :] % extent == index[:, None]).astype(jnp.float32)
    ta = jnp.dot(table, first, precision=HI)
    tb = jnp.dot(table, second, precision=HI)
    return (ta[:, None, :] * tb[None, :, :]).reshape(extent * extent, -1)


def cas_three(field, table):
    field = jnp.einsum("absc,ck->absk", field, table, precision=MID)
    field = jnp.einsum("absc,kb->aksc", field, table, precision=MID)
    return jnp.einsum("absc,ka->kbsc", field, table, precision=MID)


def make_local(n_grp_bands, n_grp, n_col):
    def local(orbitals, column_cell, column_length, sources, weights):
        extent = GRID
        count = column_cell.shape[0]
        width = orbitals.shape[1]
        depth = width * n_col // count
        n_src = sources.shape[0]

        g = lax.axis_index("grp")
        owner = sources // n_grp_bands
        rows = (sources % n_grp_bands)[:, None] == jnp.arange(n_grp_bands, dtype=jnp.int32)[None, :]
        picked = jnp.dot(rows.astype(jnp.float32), orbitals, precision=HI)
        picked = jnp.where((owner == g)[:, None], picked, 0.0)
        spread = jnp.broadcast_to(picked[None], (n_grp, n_src, width))
        picked = jnp.sum(lax.all_to_all(spread, "grp", 0, 0, tiled=True), axis=0)
        send = jnp.concatenate(
            [orbitals[:, None, :], jnp.broadcast_to(picked[None], (n_grp_bands, n_src, width))], axis=1)
        send, column_cell, column_length = lax.optimization_barrier((send, column_cell, column_length))
        got = lax.all_to_all(send, "col", 0, 0, tiled=True)
        table = cas_matrix(extent) + 0.0 * column_length[0]
        kernel = kernel_grid(extent)
        cos_h, sin_h, live = shift_tables(column_length, depth, extent)
        slot = jnp.arange(depth, dtype=jnp.int32)
        fwd = jnp.concatenate([table[:depth], table[(extent - slot) % extent]], axis=1)
        bwd = jnp.concatenate([table[:, :depth], table[:, (extent - slot) % extent]], axis=0)
        w = lax.optimization_barrier(plane_matrix(column_cell, table, extent))
        n = 1 + n_src
        coeff = got.reshape(n_col, n, width // depth, depth).transpose(0, 2, 1, 3).reshape(count, n, depth)
        coeff = jnp.where(live[:, None, :], coeff, 0.0)
        both = jnp.dot(coeff.reshape(count * n, depth), fwd, precision=HI).reshape(count, n, 2, extent)
        cols = cos_h[:, None, :] * both[:, :, 0] - sin_h[:, None, :] * both[:, :, 1]
        grids = jnp.dot(w, cols.reshape(count, n * extent), precision=HI)
        grids = grids.reshape(extent, extent, n, extent)
        own = grids[:, :, :1]
        src = grids[:, :, 1:]
        density = own * src
        potential = cas_three(kernel[:, :, None, :] * cas_three(density, table), table)
        total = jnp.sum(weights[None, None, :, None] * potential * src, axis=2)
        back = lax.dot_general(w, total.reshape(extent * extent, extent), (((0,), (0,)), ((), ())), precision=HI)
        scaled = jnp.concatenate([back * cos_h, -(back * sin_h)], axis=1)
        out = -jnp.dot(scaled, bwd, precision=HI)
        out = jnp.where(live, out, 0.0)
        return lax.all_to_all(out.reshape(n_col, 1, width), "col", 0, 0, tiled=True).reshape(n_col, width)

    return local


def solution(mesh):
    n_grp = mesh.shape["grp"]
    n_col = mesh.shape["col"]

    def run(orbitals, column_cell, column_length, sources, weights):
        n_grp_bands = orbitals.shape[0] // n_grp
        body = make_local(n_grp_bands, n_grp, n_col)
        return jax.shard_map(
            body,
            mesh=mesh,
            in_specs=(P("grp", "col"), P(), P(), P(), P()),
            out_specs=P("grp", "col"),
            check_vma=False,
        )(orbitals, column_cell, column_length, sources, weights)

    return run
```

```python
import math

import jax
import jax.numpy as jnp
from jax import lax
from jax.sharding import PartitionSpec as P

GRID = 48

kernel_scale = 20000.0
screen_shift = 4.0

HI = lax.Precision.HIGHEST
MID = lax.Precision.HIGH


def cas_matrix(extent):
    index = jnp.arange(extent, dtype=jnp.int32)
    phase = index[:, None] * index[None, :] % extent
    angle = phase.astype(jnp.float32) * (2.0 * math.pi / extent)
    return (jnp.cos(angle) + jnp.sin(angle)) / math.sqrt(extent)


def kernel_grid(extent):
    index = jnp.arange(extent, dtype=jnp.int32)
    freq = jnp.minimum(index, extent - index)
    square = freq * freq
    total = square[:, None, None] + square[None, :, None] + square[None, None, :]
    kernel = kernel_scale / (total.astype(jnp.float32) + screen_shift)
    return jnp.where(total > 0, kernel, 0.0)


def shift_tables(column_length, depth, extent):
    half = column_length // 2
    index = jnp.arange(extent, dtype=jnp.int32)
    phase = (half[:, None] * index[None, :]) % extent
    angle = phase.astype(jnp.float32) * (2.0 * math.pi / extent)
    slot = jnp.arange(depth, dtype=jnp.int32)
    live = slot[None, :] < column_length[:, None]
    return jnp.cos(angle), jnp.sin(angle), live


def plane_matrix(column_cell, table, extent):
    index = jnp.arange(extent, dtype=jnp.int32)
    first = (column_cell[None, :] // extent == index[:, None]).astype(jnp.float32)
    second = (column_cell[None, :] % extent == index[:, None]).astype(jnp.float32)
    ta = jnp.dot(table, first, precision=HI)
    tb = jnp.dot(table, second, precision=HI)
    return (ta[:, None, :] * tb[None, :, :]).reshape(extent * extent, -1)


def cas_three(field, table):
    field = jnp.einsum("absc,ck->absk", field, table, precision=MID)
    field = jnp.einsum("absc,kb->aksc", field, table, precision=MID)
    return jnp.einsum("absc,ka->kbsc", field, table, precision=MID)


def make_local(n_grp_bands, n_grp, n_col):
    def local(orbitals, column_cell, column_length, sources, weights):
        extent = GRID
        count = column_cell.shape[0]
        width = orbitals.shape[1]
        depth = width * n_col // count
        n_src = sources.shape[0]

        g = lax.axis_index("grp")
        owner = sources // n_grp_bands
        rows = (sources % n_grp_bands)[:, None] == jnp.arange(n_grp_bands, dtype=jnp.int32)[None, :]
        picked = jnp.dot(rows.astype(jnp.float32), orbitals, precision=HI)
        picked = jnp.where((owner == g)[:, None], picked, 0.0)
        spread = jnp.broadcast_to(picked[None], (n_grp, n_src, width))
        picked = jnp.sum(lax.all_to_all(spread, "grp", 0, 0, tiled=True), axis=0)
        send = jnp.concatenate(
            [orbitals[:, None, :], jnp.broadcast_to(picked[None], (n_grp_bands, n_src, width))], axis=1)
        send, column_cell, column_length = lax.optimization_barrier((send, column_cell, column_length))
        got = lax.all_to_all(send, "col", 0, 0, tiled=True)
        table = cas_matrix(extent) + 0.0 * column_length[0]
        kernel = kernel_grid(extent)
        cos_h, sin_h, live = shift_tables(column_length, depth, extent)
        slot = jnp.arange(depth, dtype=jnp.int32)
        fwd = jnp.concatenate([table[:depth], table[(extent - slot) % extent]], axis=1)
        bwd = jnp.concatenate([table[:, :depth], table[:, (extent - slot) % extent]], axis=0)
        w = lax.optimization_barrier(plane_matrix(column_cell, table, extent))
        n = 1 + n_src
        coeff = got.reshape(n_col, n, width // depth, depth).transpose(0, 2, 1, 3).reshape(count, n, depth)
        coeff = jnp.where(live[:, None, :], coeff, 0.0)
        both = jnp.dot(coeff.reshape(count * n, depth), fwd, precision=HI).reshape(count, n, 2, extent)
        cols = cos_h[:, None, :] * both[:, :, 0] - sin_h[:, None, :] * both[:, :, 1]
        grids = jnp.dot(w, cols.reshape(count, n * extent), precision=MID)
        grids = grids.reshape(extent, extent, n, extent)
        own = grids[:, :, :1]
        src = grids[:, :, 1:]
        density = own * src
        potential = cas_three(kernel[:, :, None, :] * cas_three(density, table), table)
        total = jnp.sum(weights[None, None, :, None] * potential * src, axis=2)
        back = lax.dot_general(w, total.reshape(extent * extent, extent), (((0,), (0,)), ((), ())), precision=MID)
        scaled = jnp.concatenate([back * cos_h, -(back * sin_h)], axis=1)
        out = -jnp.dot(scaled, bwd, precision=HI)
        out = jnp.where(live, out, 0.0)
        return lax.all_to_all(out.reshape(n_col, 1, width), "col", 0, 0, tiled=True).reshape(n_col, width)

    return local


def solution(mesh):
    n_grp = mesh.shape["grp"]
    n_col = mesh.shape["col"]

    def run(orbitals, column_cell, column_length, sources, weights):
        n_grp_bands = orbitals.shape[0] // n_grp
        body = make_local(n_grp_bands, n_grp, n_col)
        return jax.shard_map(
            body,
            mesh=mesh,
            in_specs=(P("grp", "col"), P(), P(), P(), P()),
            out_specs=P("grp", "col"),
            check_vma=False,
        )(orbitals, column_cell, column_length, sources, weights)

    return run
```

```python
import math

import jax
import jax.numpy as jnp
from jax import lax
from jax.sharding import PartitionSpec as P

GRID = 48

kernel_scale = 20000.0
screen_shift = 4.0

HI = lax.Precision.HIGHEST
MID = lax.Precision.HIGH


def cas_matrix(extent):
    index = jnp.arange(extent, dtype=jnp.int32)
    phase = index[:, None] * index[None, :] % extent
    angle = phase.astype(jnp.float32) * (2.0 * math.pi / extent)
    return (jnp.cos(angle) + jnp.sin(angle)) / math.sqrt(extent)


def kernel_grid(extent):
    index = jnp.arange(extent, dtype=jnp.int32)
    freq = jnp.minimum(index, extent - index)
    square = freq * freq
    total = square[:, None, None] + square[None, :, None] + square[None, None, :]
    kernel = kernel_scale / (total.astype(jnp.float32) + screen_shift)
    return jnp.where(total > 0, kernel, 0.0)


def shift_tables(column_length, depth, extent):
    half = column_length // 2
    index = jnp.arange(extent, dtype=jnp.int32)
    phase = (half[:, None] * index[None, :]) % extent
    angle = phase.astype(jnp.float32) * (2.0 * math.pi / extent)
    slot = jnp.arange(depth, dtype=jnp.int32)
    live = slot[None, :] < column_length[:, None]
    return jnp.cos(angle), jnp.sin(angle), live


def plane_matrix(column_cell, table, extent):
    index = jnp.arange(extent, dtype=jnp.int32)
    first = (column_cell[None, :] // extent == index[:, None]).astype(jnp.float32)
    second = (column_cell[None, :] % extent == index[:, None]).astype(jnp.float32)
    ta = jnp.dot(table, first, precision=HI)
    tb = jnp.dot(table, second, precision=HI)
    return (ta[:, None, :] * tb[None, :, :]).reshape(extent * extent, -1)


def cas_three(field, table):
    field = jnp.einsum("absc,ck->absk", field, table, precision=MID)
    field = jnp.einsum("absc,kb->aksc", field, table, precision=MID)
    return jnp.einsum("absc,ka->kbsc", field, table, precision=MID)


def make_local(n_grp_bands, n_grp, n_col):
    def local(orbitals, column_cell, column_length, sources, weights):
        extent = GRID
        count = column_cell.shape[0]
        width = orbitals.shape[1]
        depth = width * n_col // count
        n_src = sources.shape[0]

        g = lax.axis_index("grp")
        owner = sources // n_grp_bands
        rows = (sources % n_grp_bands)[:, None] == jnp.arange(n_grp_bands, dtype=jnp.int32)[None, :]
        picked = jnp.dot(rows.astype(jnp.float32), orbitals, precision=HI)
        picked = jnp.where((owner == g)[:, None], picked, 0.0)
        spread = jnp.broadcast_to(picked[None], (n_grp, n_src, width))
        picked = jnp.sum(lax.all_to_all(spread, "grp", 0, 0, tiled=True), axis=0)
        send = jnp.concatenate(
            [orbitals[:, None, :], jnp.broadcast_to(picked[None], (n_grp_bands, n_src, width))], axis=1)
        send, column_cell, column_length = lax.optimization_barrier((send, column_cell, column_length))
        got = lax.all_to_all(send, "col", 0, 0, tiled=True)
        table = cas_matrix(extent)
        kernel = kernel_grid(extent)
        cos_h, sin_h, live = shift_tables(column_length, depth, extent)
        slot = jnp.arange(depth, dtype=jnp.int32)
        fwd = jnp.concatenate([table[:depth], table[(extent - slot) % extent]], axis=1)
        bwd = jnp.concatenate([table[:, :depth], table[:, (extent - slot) % extent]], axis=0)
        w = lax.optimization_barrier(plane_matrix(column_cell, table, extent))
        n = 1 + n_src
        coeff = got.reshape(n_col, n, width // depth, depth).transpose(0, 2, 1, 3).reshape(count, n, depth)
        coeff = jnp.where(live[:, None, :], coeff, 0.0)
        both = jnp.dot(coeff.reshape(count * n, depth), fwd, precision=HI).reshape(count, n, 2, extent)
        cols = cos_h[:, None, :] * both[:, :, 0] - sin_h[:, None, :] * both[:, :, 1]
        grids = jnp.dot(w, cols.reshape(count, n * extent), precision=MID)
        grids = grids.reshape(extent, extent, n, extent)
        own = grids[:, :, :1]
        src = grids[:, :, 1:]
        density = own * src
        potential = cas_three(kernel[:, :, None, :] * cas_three(density, table), table)
        total = jnp.sum(weights[None, None, :, None] * potential * src, axis=2)
        back = lax.dot_general(w, total.reshape(extent * extent, extent), (((0,), (0,)), ((), ())), precision=MID)
        scaled = jnp.concatenate([back * cos_h, -(back * sin_h)], axis=1)
        out = -jnp.dot(scaled, bwd, precision=HI)
        out = jnp.where(live, out, 0.0)
        return lax.all_to_all(out.reshape(n_col, 1, width), "col", 0, 0, tiled=True).reshape(n_col, width)

    return local


def solution(mesh):
    n_grp = mesh.shape["grp"]
    n_col = mesh.shape["col"]

    def run(orbitals, column_cell, column_length, sources, weights):
        n_grp_bands = orbitals.shape[0] // n_grp
        body = make_local(n_grp_bands, n_grp, n_col)
        return jax.shard_map(
            body,
            mesh=mesh,
            in_specs=(P("grp", "col"), P(), P(), P(), P()),
            out_specs=P("grp", "col"),
            check_vma=False,
        )(orbitals, column_cell, column_length, sources, weights)

    return run
```

```python
import math

import jax
import jax.numpy as jnp
from jax import lax
from jax.sharding import PartitionSpec as P

GRID = 48

kernel_scale = 20000.0
screen_shift = 4.0

HI = lax.Precision.HIGHEST
MID = lax.Precision.HIGH


def cas_matrix(extent):
    index = jnp.arange(extent, dtype=jnp.int32)
    phase = index[:, None] * index[None, :] % extent
    angle = phase.astype(jnp.float32) * (2.0 * math.pi / extent)
    return (jnp.cos(angle) + jnp.sin(angle)) / math.sqrt(extent)


def kernel_grid(extent):
    index = jnp.arange(extent, dtype=jnp.int32)
    freq = jnp.minimum(index, extent - index)
    square = freq * freq
    total = square[:, None, None] + square[None, :, None] + square[None, None, :]
    kernel = kernel_scale / (total.astype(jnp.float32) + screen_shift)
    return jnp.where(total > 0, kernel, 0.0)


def shift_tables(column_length, depth, extent):
    half = column_length // 2
    index = jnp.arange(extent, dtype=jnp.int32)
    phase = (half[:, None] * index[None, :]) % extent
    angle = phase.astype(jnp.float32) * (2.0 * math.pi / extent)
    slot = jnp.arange(depth, dtype=jnp.int32)
    live = slot[None, :] < column_length[:, None]
    return jnp.cos(angle), jnp.sin(angle), live


def plane_matrix(column_cell, table, extent):
    index = jnp.arange(extent, dtype=jnp.int32)
    first = (column_cell[None, :] // extent == index[:, None]).astype(jnp.float32)
    second = (column_cell[None, :] % extent == index[:, None]).astype(jnp.float32)
    ta = jnp.dot(table, first, precision=HI)
    tb = jnp.dot(table, second, precision=HI)
    return (ta[:, None, :] * tb[None, :, :]).reshape(extent * extent, -1)


def cas_three(field, table):
    field = jnp.einsum("absc,ck->absk", field, table, precision=MID)
    field = jnp.einsum("absc,kb->aksc", field, table, precision=MID)
    return jnp.einsum("absc,ka->kbsc", field, table, precision=MID)


def make_local(n_grp_bands, n_grp, n_col):
    def local(orbitals, column_cell, column_length, sources, weights):
        extent = GRID
        count = column_cell.shape[0]
        width = orbitals.shape[1]
        depth = width * n_col // count
        n_src = sources.shape[0]

        g = lax.axis_index("grp")
        owner = lax.div(sources, jnp.int32(n_grp_bands))
        local_row = lax.rem(sources, jnp.int32(n_grp_bands))
        rows = (local_row[:, None] == jnp.arange(n_grp_bands, dtype=jnp.int32)[None, :]) & (owner == g)[:, None]
        picked = jnp.dot(rows.astype(jnp.float32), orbitals, precision=HI)
        spread = jnp.broadcast_to(picked[None], (n_grp, n_src, width))
        picked = jnp.sum(lax.all_to_all(spread, "grp", 0, 0, tiled=True), axis=0)
        send = jnp.concatenate(
            [orbitals[:, None, :], jnp.broadcast_to(picked[None], (n_grp_bands, n_src, width))], axis=1)
        send, column_cell, column_length = lax.optimization_barrier((send, column_cell, column_length))
        got = lax.all_to_all(send, "col", 0, 0, tiled=True)
        table = cas_matrix(extent)
        kernel = kernel_grid(extent)
        cos_h, sin_h, live = shift_tables(column_length, depth, extent)
        slot = jnp.arange(depth, dtype=jnp.int32)
        fwd = jnp.concatenate([table[:depth], table[(extent - slot) % extent]], axis=1)
        bwd = jnp.concatenate([table[:, :depth], table[:, (extent - slot) % extent]], axis=0)
        w = lax.optimization_barrier(plane_matrix(column_cell, table, extent))
        n = 1 + n_src
        coeff = got.reshape(n_col, n, width // depth, depth).transpose(0, 2, 1, 3).reshape(count, n, depth)
        coeff = jnp.where(live[:, None, :], coeff, 0.0)
        both = jnp.dot(coeff.reshape(count * n, depth), fwd, precision=HI).reshape(count, n, 2, extent)
        cols = cos_h[:, None, :] * both[:, :, 0] - sin_h[:, None, :] * both[:, :, 1]
        grids = jnp.dot(w, cols.reshape(count, n * extent), precision=MID)
        grids = grids.reshape(extent, extent, n, extent)
        own = grids[:, :, :1]
        src = grids[:, :, 1:]
        density = own * src
        potential = cas_three(kernel[:, :, None, :] * cas_three(density, table), table)
        total = jnp.sum(weights[None, None, :, None] * potential * src, axis=2)
        back = lax.dot_general(w, total.reshape(extent * extent, extent), (((0,), (0,)), ((), ())), precision=MID)
        scaled = jnp.concatenate([back * cos_h, -(back * sin_h)], axis=1)
        out = -jnp.dot(scaled, bwd, precision=HI)
        out = jnp.where(live, out, 0.0)
        return lax.all_to_all(out.reshape(n_col, 1, width), "col", 0, 0, tiled=True).reshape(n_col, width)

    return local


def solution(mesh):
    n_grp = mesh.shape["grp"]
    n_col = mesh.shape["col"]

    def run(orbitals, column_cell, column_length, sources, weights):
        n_grp_bands = orbitals.shape[0] // n_grp
        body = make_local(n_grp_bands, n_grp, n_col)
        return jax.shard_map(
            body,
            mesh=mesh,
            in_specs=(P("grp", "col"), P(), P(), P(), P()),
            out_specs=P("grp", "col"),
            check_vma=False,
        )(orbitals, column_cell, column_length, sources, weights)

    return run
```

```python
import math

import jax
import jax.numpy as jnp
from jax import lax
from jax.sharding import PartitionSpec as P

GRID = 48

kernel_scale = 20000.0
screen_shift = 4.0

HI = lax.Precision.HIGHEST
MID = lax.Precision.HIGH


def cas_matrix(extent):
    index = jnp.arange(extent, dtype=jnp.int32)
    phase = index[:, None] * index[None, :] % extent
    angle = phase.astype(jnp.float32) * (2.0 * math.pi / extent)
    return (jnp.cos(angle) + jnp.sin(angle)) / math.sqrt(extent)


def kernel_grid(extent):
    index = jnp.arange(extent, dtype=jnp.int32)
    freq = jnp.minimum(index, extent - index)
    square = freq * freq
    total = square[:, None, None] + square[None, :, None] + square[None, None, :]
    kernel = kernel_scale / (total.astype(jnp.float32) + screen_shift)
    return jnp.where(total > 0, kernel, 0.0)


def shift_tables(column_length, depth, extent):
    half = column_length // 2
    index = jnp.arange(extent, dtype=jnp.int32)
    phase = (half[:, None] * index[None, :]) % extent
    angle = phase.astype(jnp.float32) * (2.0 * math.pi / extent)
    slot = jnp.arange(depth, dtype=jnp.int32)
    live = slot[None, :] < column_length[:, None]
    return jnp.cos(angle), jnp.sin(angle), live


def plane_matrix(column_cell, table, extent):
    index = jnp.arange(extent, dtype=jnp.int32)
    first = (column_cell[None, :] // extent == index[:, None]).astype(jnp.float32)
    second = (column_cell[None, :] % extent == index[:, None]).astype(jnp.float32)
    ta = jnp.dot(table, first, precision=HI)
    tb = jnp.dot(table, second, precision=HI)
    return (ta[:, None, :] * tb[None, :, :]).reshape(extent * extent, -1)


def cas_three(field, table):
    field = jnp.einsum("absc,ck->absk", field, table, precision=MID)
    field = jnp.einsum("absc,kb->aksc", field, table, precision=MID)
    return jnp.einsum("absc,ka->kbsc", field, table, precision=MID)


def make_local(n_grp_bands, n_grp, n_col):
    def local(orbitals, column_cell, column_length, sources, weights):
        extent = GRID
        count = column_cell.shape[0]
        width = orbitals.shape[1]
        depth = width * n_col // count
        n_src = sources.shape[0]

        g = lax.axis_index("grp")
        owner = sources // n_grp_bands
        rows = (sources % n_grp_bands)[:, None] == jnp.arange(n_grp_bands, dtype=jnp.int32)[None, :]
        picked = jnp.dot(rows.astype(jnp.float32), orbitals, precision=HI)
        picked = jnp.where((owner == g)[:, None], picked, 0.0)
        spread = jnp.broadcast_to(picked[None], (n_grp, n_src, width))
        picked = jnp.sum(lax.all_to_all(spread, "grp", 0, 0, tiled=True), axis=0)
        send = jnp.concatenate(
            [orbitals[:, None, :], jnp.broadcast_to(picked[None], (n_grp_bands, n_src, width))], axis=1)
        per_dev = count // n_col
        mine = lax.dynamic_slice_in_dim(column_length, lax.axis_index("col") * per_dev, per_dev)
        live_mine = (jnp.arange(depth, dtype=jnp.int32)[None, :] < mine[:, None]).reshape(-1)
        send = jnp.where(live_mine[None, None, :], send, 0.0)
        send, column_cell, column_length = lax.optimization_barrier((send, column_cell, column_length))
        got = lax.all_to_all(send, "col", 0, 0, tiled=True)
        table = cas_matrix(extent)
        kernel = kernel_grid(extent)
        cos_h, sin_h, live = shift_tables(column_length, depth, extent)
        slot = jnp.arange(depth, dtype=jnp.int32)
        fwd = jnp.concatenate([table[:depth], table[(extent - slot) % extent]], axis=1)
        bwd = jnp.concatenate([table[:, :depth], table[:, (extent - slot) % extent]], axis=0)
        w = lax.optimization_barrier(plane_matrix(column_cell, table, extent))
        n = 1 + n_src
        coeff = got.reshape(n_col, n, width // depth, depth).transpose(0, 2, 1, 3).reshape(count, n, depth)
        both = jnp.dot(coeff.reshape(count * n, depth), fwd, precision=HI).reshape(count, n, 2, extent)
        cols = cos_h[:, None, :] * both[:, :, 0] - sin_h[:, None, :] * both[:, :, 1]
        grids = jnp.dot(w, cols.reshape(count, n * extent), precision=MID)
        grids = grids.reshape(extent, extent, n, extent)
        own = grids[:, :, :1]
        src = grids[:, :, 1:]
        density = own * src
        potential = cas_three(kernel[:, :, None, :] * cas_three(density, table), table)
        total = jnp.sum(weights[None, None, :, None] * potential * src, axis=2)
        back = lax.dot_general(w, total.reshape(extent * extent, extent), (((0,), (0,)), ((), ())), precision=MID)
        scaled = jnp.concatenate([back * cos_h, -(back * sin_h)], axis=1)
        out = -jnp.dot(scaled, bwd, precision=HI)
        out = jnp.where(live, out, 0.0)
        return lax.all_to_all(out.reshape(n_col, width), "col", 0, 0, tiled=True)

    return local


def solution(mesh):
    n_grp = mesh.shape["grp"]
    n_col = mesh.shape["col"]

    def run(orbitals, column_cell, column_length, sources, weights):
        n_grp_bands = orbitals.shape[0] // n_grp
        body = make_local(n_grp_bands, n_grp, n_col)
        return jax.shard_map(
            body,
            mesh=mesh,
            in_specs=(P("grp", "col"), P(), P(), P(), P()),
            out_specs=P("grp", "col"),
            check_vma=False,
        )(orbitals, column_cell, column_length, sources, weights)

    return run
```

```python
import math

import jax
import jax.numpy as jnp
from jax import lax
from jax.sharding import PartitionSpec as P

GRID = 48

kernel_scale = 20000.0
screen_shift = 4.0

HI = lax.Precision.HIGHEST
MID = lax.Precision.HIGH


def cas_matrix(extent):
    index = jnp.arange(extent, dtype=jnp.int32)
    phase = index[:, None] * index[None, :] % extent
    angle = phase.astype(jnp.float32) * (2.0 * math.pi / extent)
    return (jnp.cos(angle) + jnp.sin(angle)) / math.sqrt(extent)


def kernel_grid(extent):
    index = jnp.arange(extent, dtype=jnp.int32)
    freq = jnp.minimum(index, extent - index)
    square = freq * freq
    total = square[:, None, None] + square[None, :, None] + square[None, None, :]
    kernel = kernel_scale / (total.astype(jnp.float32) + screen_shift)
    return jnp.where(total > 0, kernel, 0.0)


def shift_tables(column_length, depth, extent):
    half = column_length // 2
    index = jnp.arange(extent, dtype=jnp.int32)
    phase = (half[:, None] * index[None, :]) % extent
    angle = phase.astype(jnp.float32) * (2.0 * math.pi / extent)
    slot = jnp.arange(depth, dtype=jnp.int32)
    live = slot[None, :] < column_length[:, None]
    return jnp.cos(angle), jnp.sin(angle), live


def plane_matrix(column_cell, table, extent):
    index = jnp.arange(extent, dtype=jnp.int32)
    first = (column_cell[None, :] // extent == index[:, None]).astype(jnp.float32)
    second = (column_cell[None, :] % extent == index[:, None]).astype(jnp.float32)
    ta = jnp.dot(table, first, precision=HI)
    tb = jnp.dot(table, second, precision=HI)
    return (ta[:, None, :] * tb[None, :, :]).reshape(extent * extent, -1)


def cas_three(field, table):
    field = jnp.einsum("absc,ck->absk", field, table, precision=MID)
    field = jnp.einsum("absc,kb->aksc", field, table, precision=MID)
    return jnp.einsum("absc,ka->kbsc", field, table, precision=MID)


def make_local(n_grp_bands, n_grp, n_col):
    def local(orbitals, column_cell, column_length, sources, weights):
        extent = GRID
        count = column_cell.shape[0]
        width = orbitals.shape[1]
        depth = width * n_col // count
        n_src = sources.shape[0]

        everyone = lax.all_to_all(jnp.broadcast_to(orbitals[None], (n_grp,) + orbitals.shape), "grp", 0, 0, tiled=True)
        everyone = everyone.reshape(n_grp * n_grp_bands, width)
        rows = sources[:, None] == jnp.arange(n_grp * n_grp_bands, dtype=jnp.int32)[None, :]
        picked = jnp.dot(rows.astype(jnp.float32), everyone, precision=HI)
        send = jnp.concatenate(
            [orbitals[:, None, :], jnp.broadcast_to(picked[None], (n_grp_bands, n_src, width))], axis=1)
        send, column_cell, column_length = lax.optimization_barrier((send, column_cell, column_length))
        got = lax.all_to_all(send, "col", 0, 0, tiled=True)
        table = cas_matrix(extent)
        kernel = kernel_grid(extent)
        cos_h, sin_h, live = shift_tables(column_length, depth, extent)
        slot = jnp.arange(depth, dtype=jnp.int32)
        fwd = jnp.concatenate([table[:depth], table[(extent - slot) % extent]], axis=1)
        bwd = jnp.concatenate([table[:, :depth], table[:, (extent - slot) % extent]], axis=0)
        w = lax.optimization_barrier(plane_matrix(column_cell, table, extent))
        n = 1 + n_src
        coeff = got.reshape(n_col, n, width // depth, depth).transpose(0, 2, 1, 3).reshape(count, n, depth)
        coeff = jnp.where(live[:, None, :], coeff, 0.0)
        both = jnp.dot(coeff.reshape(count * n, depth), fwd, precision=HI).reshape(count, n, 2, extent)
        cols = cos_h[:, None, :] * both[:, :, 0] - sin_h[:, None, :] * both[:, :, 1]
        grids = jnp.dot(w, cols.reshape(count, n * extent), precision=MID)
        grids = grids.reshape(extent, extent, n, extent)
        own = grids[:, :, :1]
        src = grids[:, :, 1:]
        density = own * src
        potential = cas_three(kernel[:, :, None, :] * cas_three(density, table), table)
        total = jnp.sum(weights[None, None, :, None] * potential * src, axis=2)
        back = lax.dot_general(w, total.reshape(extent * extent, extent), (((0,), (0,)), ((), ())), precision=MID)
        scaled = jnp.concatenate([back * cos_h, -(back * sin_h)], axis=1)
        out = -jnp.dot(scaled, bwd, precision=HI)
        out = jnp.where(live, out, 0.0)
        return lax.all_to_all(out.reshape(n_col, 1, width), "col", 0, 0, tiled=True).reshape(n_col, width)

    return local


def solution(mesh):
    n_grp = mesh.shape["grp"]
    n_col = mesh.shape["col"]

    def run(orbitals, column_cell, column_length, sources, weights):
        n_grp_bands = orbitals.shape[0] // n_grp
        body = make_local(n_grp_bands, n_grp, n_col)
        return jax.shard_map(
            body,
            mesh=mesh,
            in_specs=(P("grp", "col"), P(), P(), P(), P()),
            out_specs=P("grp", "col"),
            check_vma=False,
        )(orbitals, column_cell, column_length, sources, weights)

    return run
```

```python
import math

import jax
import jax.numpy as jnp
from jax import lax
from jax.sharding import PartitionSpec as P

GRID = 48

kernel_scale = 20000.0
screen_shift = 4.0

HI = lax.Precision.HIGHEST
MID = lax.Precision.HIGH


def cas_matrix(extent):
    index = jnp.arange(extent, dtype=jnp.int32)
    phase = index[:, None] * index[None, :] % extent
    angle = phase.astype(jnp.float32) * (2.0 * math.pi / extent)
    return (jnp.cos(angle) + jnp.sin(angle)) / math.sqrt(extent)


def kernel_grid(extent):
    index = jnp.arange(extent, dtype=jnp.int32)
    freq = jnp.minimum(index, extent - index)
    square = freq * freq
    total = square[:, None, None] + square[None, :, None] + square[None, None, :]
    kernel = kernel_scale / (total.astype(jnp.float32) + screen_shift)
    return jnp.where(total > 0, kernel, 0.0)


def shift_tables(column_length, depth, extent):
    half = column_length // 2
    index = jnp.arange(extent, dtype=jnp.int32)
    phase = (half[:, None] * index[None, :]) % extent
    angle = phase.astype(jnp.float32) * (2.0 * math.pi / extent)
    slot = jnp.arange(depth, dtype=jnp.int32)
    live = slot[None, :] < column_length[:, None]
    return jnp.cos(angle), jnp.sin(angle), live


def plane_matrix(column_cell, table, extent):
    index = jnp.arange(extent, dtype=jnp.int32)
    first = (column_cell[None, :] // extent == index[:, None]).astype(jnp.float32)
    second = (column_cell[None, :] % extent == index[:, None]).astype(jnp.float32)
    ta = jnp.dot(table, first, precision=HI)
    tb = jnp.dot(table, second, precision=HI)
    return (ta[:, None, :] * tb[None, :, :]).reshape(extent * extent, -1)


def cas_three(field, table):
    field = jnp.einsum("absc,ck->absk", field, table, precision=MID)
    field = jnp.einsum("absc,kb->aksc", field, table, precision=MID)
    return jnp.einsum("absc,ka->kbsc", field, table, precision=MID)


def cas_three_reversed(field, table):
    field = jnp.einsum("absc,ka->kbsc", field, table, precision=MID)
    field = jnp.einsum("absc,kb->aksc", field, table, precision=MID)
    return jnp.einsum("absc,ck->absk", field, table, precision=MID)


def make_local(n_grp_bands, n_grp, n_col):
    def local(orbitals, column_cell, column_length, sources, weights):
        extent = GRID
        count = column_cell.shape[0]
        width = orbitals.shape[1]
        depth = width * n_col // count
        n_src = sources.shape[0]

        g = lax.axis_index("grp")
        owner = sources // n_grp_bands
        rows = (sources % n_grp_bands)[:, None] == jnp.arange(n_grp_bands, dtype=jnp.int32)[None, :]
        picked = jnp.dot(rows.astype(jnp.float32), orbitals, precision=HI)
        picked = jnp.where((owner == g)[:, None], picked, 0.0)
        spread = jnp.broadcast_to(picked[None], (n_grp, n_src, width))
        picked = jnp.sum(lax.all_to_all(spread, "grp", 0, 0, tiled=True), axis=0)
        send = jnp.concatenate(
            [orbitals[:, None, :], jnp.broadcast_to(picked[None], (n_grp_bands, n_src, width))], axis=1)
        send, column_cell, column_length = lax.optimization_barrier((send, column_cell, column_length))
        got = lax.all_to_all(send, "col", 0, 0, tiled=True)
        table = cas_matrix(extent)
        kernel = kernel_grid(extent)
        cos_h, sin_h, live = shift_tables(column_length, depth, extent)
        slot = jnp.arange(depth, dtype=jnp.int32)
        fwd = jnp.concatenate([table[:depth], table[(extent - slot) % extent]], axis=1)
        bwd = jnp.concatenate([table[:, :depth], table[:, (extent - slot) % extent]], axis=0)
        w = lax.optimization_barrier(plane_matrix(column_cell, table, extent))
        n = 1 + n_src
        coeff = got.reshape(n_col, n, width // depth, depth).transpose(0, 2, 1, 3).reshape(count, n, depth)
        coeff = jnp.where(live[:, None, :], coeff, 0.0)
        both = jnp.dot(coeff.reshape(count * n, depth), fwd, precision=HI).reshape(count, n, 2, extent)
        cols = cos_h[:, None, :] * both[:, :, 0] - sin_h[:, None, :] * both[:, :, 1]
        grids = jnp.dot(w, cols.reshape(count, n * extent), precision=MID)
        grids = grids.reshape(extent, extent, n, extent)
        own = grids[:, :, :1]
        src = grids[:, :, 1:]
        density = own * src
        potential = cas_three_reversed(kernel[:, :, None, :] * cas_three(density, table), table)
        total = jnp.sum(weights[None, None, :, None] * potential * src, axis=2)
        back = lax.dot_general(w, total.reshape(extent * extent, extent), (((0,), (0,)), ((), ())), precision=MID)
        scaled = jnp.concatenate([back * cos_h, -(back * sin_h)], axis=1)
        out = -jnp.dot(scaled, bwd, precision=HI)
        out = jnp.where(live, out, 0.0)
        return lax.all_to_all(out.reshape(n_col, 1, width), "col", 0, 0, tiled=True).reshape(n_col, width)

    return local


def solution(mesh):
    n_grp = mesh.shape["grp"]
    n_col = mesh.shape["col"]

    def run(orbitals, column_cell, column_length, sources, weights):
        n_grp_bands = orbitals.shape[0] // n_grp
        body = make_local(n_grp_bands, n_grp, n_col)
        return jax.shard_map(
            body,
            mesh=mesh,
            in_specs=(P("grp", "col"), P(), P(), P(), P()),
            out_specs=P("grp", "col"),
            check_vma=False,
        )(orbitals, column_cell, column_length, sources, weights)

    return run
```

```python
import math

import jax
import jax.numpy as jnp
from jax import lax
from jax.sharding import PartitionSpec as P

GRID = 48

kernel_scale = 20000.0
screen_shift = 4.0

HI = lax.Precision.HIGHEST
MID = lax.Precision.HIGH


def cas_matrix(extent):
    index = jnp.arange(extent, dtype=jnp.int32)
    phase = index[:, None] * index[None, :] % extent
    angle = phase.astype(jnp.float32) * (2.0 * math.pi / extent)
    return (jnp.cos(angle) + jnp.sin(angle)) / math.sqrt(extent)


def kernel_grid(extent):
    index = jnp.arange(extent, dtype=jnp.int32)
    freq = jnp.minimum(index, extent - index)
    square = freq * freq
    total = square[:, None, None] + square[None, :, None] + square[None, None, :]
    kernel = kernel_scale / (total.astype(jnp.float32) + screen_shift)
    return jnp.where(total > 0, kernel, 0.0)


def shift_tables(column_length, depth, extent):
    half = column_length // 2
    index = jnp.arange(extent, dtype=jnp.int32)
    phase = (half[:, None] * index[None, :]) % extent
    angle = phase.astype(jnp.float32) * (2.0 * math.pi / extent)
    slot = jnp.arange(depth, dtype=jnp.int32)
    live = slot[None, :] < column_length[:, None]
    return jnp.cos(angle), jnp.sin(angle), live


def plane_matrix(column_cell, table, extent):
    index = jnp.arange(extent, dtype=jnp.int32)
    first = (column_cell[None, :] // extent == index[:, None]).astype(jnp.float32)
    second = (column_cell[None, :] % extent == index[:, None]).astype(jnp.float32)
    ta = jnp.dot(table, first, precision=HI)
    tb = jnp.dot(table, second, precision=HI)
    return (ta[:, None, :] * tb[None, :, :]).reshape(extent * extent, -1)


def cas_three(field, table):
    field = jnp.einsum("absc,ck->absk", field, table, precision=MID)
    field = jnp.einsum("absc,kb->aksc", field, table, precision=MID)
    return jnp.einsum("absc,ka->kbsc", field, table, precision=MID)


def cas_three_reversed(field, table):
    field = jnp.einsum("absc,ka->kbsc", field, table, precision=MID)
    field = jnp.einsum("absc,kb->aksc", field, table, precision=MID)
    return jnp.einsum("absc,ck->absk", field, table, precision=MID)


def make_local(n_grp_bands, n_grp, n_col):
    def local(orbitals, column_cell, column_length, sources, weights):
        extent = GRID
        count = column_cell.shape[0]
        width = orbitals.shape[1]
        depth = width * n_col // count
        n_src = sources.shape[0]

        g = lax.axis_index("grp")
        owner = sources // n_grp_bands
        rows = (sources % n_grp_bands)[:, None] == jnp.arange(n_grp_bands, dtype=jnp.int32)[None, :]
        picked = jnp.dot(rows.astype(jnp.float32), orbitals, precision=HI)
        picked = jnp.where((owner == g)[:, None], picked, 0.0)
        spread = jnp.broadcast_to(picked[None], (n_grp, n_src, width))
        picked = jnp.sum(lax.all_to_all(spread, "grp", 0, 0, tiled=True), axis=0)
        send = jnp.concatenate(
            [orbitals[:, None, :], jnp.broadcast_to(picked[None], (n_grp_bands, n_src, width))], axis=1)
        send, column_cell, column_length = lax.optimization_barrier((send, column_cell, column_length))
        got = lax.all_to_all(send, "col", 0, 0, tiled=True)
        table = cas_matrix(extent)
        kernel = kernel_grid(extent)
        cos_h, sin_h, live = shift_tables(column_length, depth, extent)
        slot = jnp.arange(depth, dtype=jnp.int32)
        fwd = jnp.concatenate([table[:depth], table[(extent - slot) % extent]], axis=1)
        bwd = jnp.concatenate([table[:, :depth], table[:, (extent - slot) % extent]], axis=0)
        w = lax.optimization_barrier(plane_matrix(column_cell, table, extent))
        n = 1 + n_src
        coeff = got.reshape(n_col, n, width // depth, depth).transpose(0, 2, 1, 3).reshape(count, n, depth)
        coeff = jnp.where(live[:, None, :], coeff, 0.0)
        both = jnp.dot(coeff.reshape(count * n, depth), fwd, precision=HI).reshape(count, n, 2, extent)
        cols = cos_h[:, None, :] * both[:, :, 0] - sin_h[:, None, :] * both[:, :, 1]
        grids = jnp.dot(w, cols.reshape(count, n * extent), precision=MID)
        grids = grids.reshape(extent, extent, n, extent)
        own = grids[:, :, :1]
        src = grids[:, :, 1:]
        density = own * src
        potential = cas_three(kernel[:, :, None, :] * cas_three_reversed(density, table), table)
        total = jnp.sum(weights[None, None, :, None] * potential * src, axis=2)
        back = lax.dot_general(w, total.reshape(extent * extent, extent), (((0,), (0,)), ((), ())), precision=MID)
        scaled = jnp.concatenate([back * cos_h, -(back * sin_h)], axis=1)
        out = -jnp.dot(scaled, bwd, precision=HI)
        out = jnp.where(live, out, 0.0)
        return lax.all_to_all(out.reshape(n_col, 1, width), "col", 0, 0, tiled=True).reshape(n_col, width)

    return local


def solution(mesh):
    n_grp = mesh.shape["grp"]
    n_col = mesh.shape["col"]

    def run(orbitals, column_cell, column_length, sources, weights):
        n_grp_bands = orbitals.shape[0] // n_grp
        body = make_local(n_grp_bands, n_grp, n_col)
        return jax.shard_map(
            body,
            mesh=mesh,
            in_specs=(P("grp", "col"), P(), P(), P(), P()),
            out_specs=P("grp", "col"),
            check_vma=False,
        )(orbitals, column_cell, column_length, sources, weights)

    return run
```

```python
import math

import jax
import jax.numpy as jnp
from jax import lax
from jax.sharding import PartitionSpec as P

GRID = 48

kernel_scale = 20000.0
screen_shift = 4.0

HI = lax.Precision.HIGHEST
MID = lax.Precision.HIGH


def cas_matrix(extent):
    index = jnp.arange(extent, dtype=jnp.int32)
    phase = index[:, None] * index[None, :] % extent
    angle = phase.astype(jnp.float32) * (2.0 * math.pi / extent)
    return (jnp.cos(angle) + jnp.sin(angle)) / math.sqrt(extent)


def kernel_grid(extent):
    index = jnp.arange(extent, dtype=jnp.int32)
    freq = jnp.minimum(index, extent - index)
    square = freq * freq
    total = square[:, None, None] + square[None, :, None] + square[None, None, :]
    kernel = kernel_scale / (total.astype(jnp.float32) + screen_shift)
    return jnp.where(total > 0, kernel, 0.0)


def shift_tables(column_length, depth, extent):
    half = column_length // 2
    index = jnp.arange(extent, dtype=jnp.int32)
    phase = (half[:, None] * index[None, :]) % extent
    angle = phase.astype(jnp.float32) * (2.0 * math.pi / extent)
    slot = jnp.arange(depth, dtype=jnp.int32)
    live = slot[None, :] < column_length[:, None]
    return jnp.cos(angle), jnp.sin(angle), live


def plane_matrix(column_cell, table, extent):
    index = jnp.arange(extent, dtype=jnp.int32)
    first = (column_cell[None, :] // extent == index[:, None]).astype(jnp.float32)
    second = (column_cell[None, :] % extent == index[:, None]).astype(jnp.float32)
    ta = jnp.dot(table, first, precision=HI)
    tb = jnp.dot(table, second, precision=HI)
    return (ta[:, None, :] * tb[None, :, :]).reshape(extent * extent, -1)


def cas_three(field, table):
    field = jnp.einsum("absc,ck->absk", field, table, precision=MID)
    field = jnp.einsum("absc,kb->aksc", field, table, precision=MID)
    return jnp.einsum("absc,ka->kbsc", field, table, precision=MID)


def cas_three_reversed(field, table):
    field = jnp.einsum("absc,ka->kbsc", field, table, precision=MID)
    field = jnp.einsum("absc,ck->absk", field, table, precision=MID)
    return jnp.einsum("absc,kb->aksc", field, table, precision=MID)


def make_local(n_grp_bands, n_grp, n_col):
    def local(orbitals, column_cell, column_length, sources, weights):
        extent = GRID
        count = column_cell.shape[0]
        width = orbitals.shape[1]
        depth = width * n_col // count
        n_src = sources.shape[0]

        g = lax.axis_index("grp")
        owner = sources // n_grp_bands
        rows = (sources % n_grp_bands)[:, None] == jnp.arange(n_grp_bands, dtype=jnp.int32)[None, :]
        picked = jnp.dot(rows.astype(jnp.float32), orbitals, precision=HI)
        picked = jnp.where((owner == g)[:, None], picked, 0.0)
        spread = jnp.broadcast_to(picked[None], (n_grp, n_src, width))
        picked = jnp.sum(lax.all_to_all(spread, "grp", 0, 0, tiled=True), axis=0)
        send = jnp.concatenate(
            [orbitals[:, None, :], jnp.broadcast_to(picked[None], (n_grp_bands, n_src, width))], axis=1)
        send, column_cell, column_length = lax.optimization_barrier((send, column_cell, column_length))
        got = lax.all_to_all(send, "col", 0, 0, tiled=True)
        table = cas_matrix(extent)
        kernel = kernel_grid(extent)
        cos_h, sin_h, live = shift_tables(column_length, depth, extent)
        slot = jnp.arange(depth, dtype=jnp.int32)
        fwd = jnp.concatenate([table[:depth], table[(extent - slot) % extent]], axis=1)
        bwd = jnp.concatenate([table[:, :depth], table[:, (extent - slot) % extent]], axis=0)
        w = lax.optimization_barrier(plane_matrix(column_cell, table, extent))
        n = 1 + n_src
        coeff = got.reshape(n_col, n, width // depth, depth).transpose(0, 2, 1, 3).reshape(count, n, depth)
        coeff = jnp.where(live[:, None, :], coeff, 0.0)
        both = jnp.dot(coeff.reshape(count * n, depth), fwd, precision=HI).reshape(count, n, 2, extent)
        cols = cos_h[:, None, :] * both[:, :, 0] - sin_h[:, None, :] * both[:, :, 1]
        grids = jnp.dot(w, cols.reshape(count, n * extent), precision=MID)
        grids = grids.reshape(extent, extent, n, extent)
        own = grids[:, :, :1]
        src = grids[:, :, 1:]
        density = own * src
        potential = cas_three_reversed(kernel[:, :, None, :] * cas_three(density, table), table)
        total = jnp.sum(weights[None, None, :, None] * potential * src, axis=2)
        back = lax.dot_general(w, total.reshape(extent * extent, extent), (((0,), (0,)), ((), ())), precision=MID)
        scaled = jnp.concatenate([back * cos_h, -(back * sin_h)], axis=1)
        out = -jnp.dot(scaled, bwd, precision=HI)
        out = jnp.where(live, out, 0.0)
        return lax.all_to_all(out.reshape(n_col, 1, width), "col", 0, 0, tiled=True).reshape(n_col, width)

    return local


def solution(mesh):
    n_grp = mesh.shape["grp"]
    n_col = mesh.shape["col"]

    def run(orbitals, column_cell, column_length, sources, weights):
        n_grp_bands = orbitals.shape[0] // n_grp
        body = make_local(n_grp_bands, n_grp, n_col)
        return jax.shard_map(
            body,
            mesh=mesh,
            in_specs=(P("grp", "col"), P(), P(), P(), P()),
            out_specs=P("grp", "col"),
            check_vma=False,
        )(orbitals, column_cell, column_length, sources, weights)

    return run
```

```python
import math

import jax
import jax.numpy as jnp
from jax import lax
from jax.sharding import PartitionSpec as P

GRID = 48

kernel_scale = 20000.0
screen_shift = 4.0

HI = lax.Precision.HIGHEST
MID = lax.Precision.HIGH


def cas_matrix(extent):
    index = jnp.arange(extent, dtype=jnp.int32)
    phase = index[:, None] * index[None, :] % extent
    angle = phase.astype(jnp.float32) * (2.0 * math.pi / extent)
    return (jnp.cos(angle) + jnp.sin(angle)) / math.sqrt(extent)


def kernel_grid(extent):
    index = jnp.arange(extent, dtype=jnp.int32)
    freq = jnp.minimum(index, extent - index)
    square = freq * freq
    total = square[:, None, None] + square[None, :, None] + square[None, None, :]
    kernel = kernel_scale / (total.astype(jnp.float32) + screen_shift)
    return jnp.where(total > 0, kernel, 0.0)


def shift_tables(column_length, depth, extent):
    half = column_length // 2
    index = jnp.arange(extent, dtype=jnp.int32)
    phase = (half[:, None] * index[None, :]) % extent
    angle = phase.astype(jnp.float32) * (2.0 * math.pi / extent)
    slot = jnp.arange(depth, dtype=jnp.int32)
    live = slot[None, :] < column_length[:, None]
    return jnp.cos(angle), jnp.sin(angle), live


def plane_matrix(column_cell, table, extent):
    index = jnp.arange(extent, dtype=jnp.int32)
    first = (column_cell[None, :] // extent == index[:, None]).astype(jnp.float32)
    second = (column_cell[None, :] % extent == index[:, None]).astype(jnp.float32)
    ta = jnp.dot(table, first, precision=HI)
    tb = jnp.dot(table, second, precision=HI)
    return (ta[:, None, :] * tb[None, :, :]).reshape(extent * extent, -1)


def cas_three(field, table):
    field = jnp.einsum("absc,ck->absk", field, table, precision=MID)
    field = jnp.einsum("absc,ka->kbsc", field, table, precision=MID)
    return jnp.einsum("absc,kb->aksc", field, table, precision=MID)


def cas_three_reversed(field, table):
    field = jnp.einsum("absc,kb->aksc", field, table, precision=MID)
    field = jnp.einsum("absc,ka->kbsc", field, table, precision=MID)
    return jnp.einsum("absc,ck->absk", field, table, precision=MID)


def make_local(n_grp_bands, n_grp, n_col):
    def local(orbitals, column_cell, column_length, sources, weights):
        extent = GRID
        count = column_cell.shape[0]
        width = orbitals.shape[1]
        depth = width * n_col // count
        n_src = sources.shape[0]

        g = lax.axis_index("grp")
        owner = sources // n_grp_bands
        rows = (sources % n_grp_bands)[:, None] == jnp.arange(n_grp_bands, dtype=jnp.int32)[None, :]
        picked = jnp.dot(rows.astype(jnp.float32), orbitals, precision=HI)
        picked = jnp.where((owner == g)[:, None], picked, 0.0)
        spread = jnp.broadcast_to(picked[None], (n_grp, n_src, width))
        picked = jnp.sum(lax.all_to_all(spread, "grp", 0, 0, tiled=True), axis=0)
        send = jnp.concatenate(
            [orbitals[:, None, :], jnp.broadcast_to(picked[None], (n_grp_bands, n_src, width))], axis=1)
        send, column_cell, column_length = lax.optimization_barrier((send, column_cell, column_length))
        got = lax.all_to_all(send, "col", 0, 0, tiled=True)
        table = cas_matrix(extent)
        kernel = kernel_grid(extent)
        cos_h, sin_h, live = shift_tables(column_length, depth, extent)
        slot = jnp.arange(depth, dtype=jnp.int32)
        fwd = jnp.concatenate([table[:depth], table[(extent - slot) % extent]], axis=1)
        bwd = jnp.concatenate([table[:, :depth], table[:, (extent - slot) % extent]], axis=0)
        w = lax.optimization_barrier(plane_matrix(column_cell, table, extent))
        n = 1 + n_src
        coeff = got.reshape(n_col, n, width // depth, depth).transpose(0, 2, 1, 3).reshape(count, n, depth)
        coeff = jnp.where(live[:, None, :], coeff, 0.0)
        both = jnp.dot(coeff.reshape(count * n, depth), fwd, precision=HI).reshape(count, n, 2, extent)
        cols = cos_h[:, None, :] * both[:, :, 0] - sin_h[:, None, :] * both[:, :, 1]
        grids = jnp.dot(w, cols.reshape(count, n * extent), precision=MID)
        grids = grids.reshape(extent, extent, n, extent)
        own = grids[:, :, :1]
        src = grids[:, :, 1:]
        density = own * src
        potential = cas_three_reversed(kernel[:, :, None, :] * cas_three(density, table), table)
        total = jnp.sum(weights[None, None, :, None] * potential * src, axis=2)
        back = lax.dot_general(w, total.reshape(extent * extent, extent), (((0,), (0,)), ((), ())), precision=MID)
        scaled = jnp.concatenate([back * cos_h, -(back * sin_h)], axis=1)
        out = -jnp.dot(scaled, bwd, precision=HI)
        out = jnp.where(live, out, 0.0)
        return lax.all_to_all(out.reshape(n_col, 1, width), "col", 0, 0, tiled=True).reshape(n_col, width)

    return local


def solution(mesh):
    n_grp = mesh.shape["grp"]
    n_col = mesh.shape["col"]

    def run(orbitals, column_cell, column_length, sources, weights):
        n_grp_bands = orbitals.shape[0] // n_grp
        body = make_local(n_grp_bands, n_grp, n_col)
        return jax.shard_map(
            body,
            mesh=mesh,
            in_specs=(P("grp", "col"), P(), P(), P(), P()),
            out_specs=P("grp", "col"),
            check_vma=False,
        )(orbitals, column_cell, column_length, sources, weights)

    return run
```

```python
import math

import jax
import jax.numpy as jnp
from jax import lax
from jax.sharding import PartitionSpec as P

GRID = 48

kernel_scale = 20000.0
screen_shift = 4.0

HI = lax.Precision.HIGHEST
MID = lax.Precision.HIGH


def cas_matrix(extent):
    index = jnp.arange(extent, dtype=jnp.int32)
    phase = index[:, None] * index[None, :] % extent
    angle = phase.astype(jnp.float32) * (2.0 * math.pi / extent)
    return (jnp.cos(angle) + jnp.sin(angle)) / math.sqrt(extent)


def kernel_grid(extent):
    index = jnp.arange(extent, dtype=jnp.int32)
    freq = jnp.minimum(index, extent - index)
    square = freq * freq
    total = square[:, None, None] + square[None, :, None] + square[None, None, :]
    kernel = kernel_scale / (total.astype(jnp.float32) + screen_shift)
    return jnp.where(total > 0, kernel, 0.0)


def shift_tables(column_length, depth, extent):
    half = column_length // 2
    index = jnp.arange(extent, dtype=jnp.int32)
    phase = (half[:, None] * index[None, :]) % extent
    angle = phase.astype(jnp.float32) * (2.0 * math.pi / extent)
    slot = jnp.arange(depth, dtype=jnp.int32)
    live = slot[None, :] < column_length[:, None]
    return jnp.cos(angle), jnp.sin(angle), live


def plane_matrix(column_cell, table, extent):
    index = jnp.arange(extent, dtype=jnp.int32)
    first = (column_cell[None, :] // extent == index[:, None]).astype(jnp.float32)
    second = (column_cell[None, :] % extent == index[:, None]).astype(jnp.float32)
    ta = jnp.dot(table, first, precision=HI)
    tb = jnp.dot(table, second, precision=HI)
    return (ta[:, None, :] * tb[None, :, :]).reshape(extent * extent, -1)


def cas_three(field, table):
    field = jnp.einsum("absc,kb->aksc", field, table, precision=MID)
    field = jnp.einsum("absc,ck->absk", field, table, precision=MID)
    return jnp.einsum("absc,ka->kbsc", field, table, precision=MID)


def cas_three_reversed(field, table):
    field = jnp.einsum("absc,ka->kbsc", field, table, precision=MID)
    field = jnp.einsum("absc,kb->aksc", field, table, precision=MID)
    return jnp.einsum("absc,ck->absk", field, table, precision=MID)


def make_local(n_grp_bands, n_grp, n_col):
    def local(orbitals, column_cell, column_length, sources, weights):
        extent = GRID
        count = column_cell.shape[0]
        width = orbitals.shape[1]
        depth = width * n_col // count
        n_src = sources.shape[0]

        g = lax.axis_index("grp")
        owner = sources // n_grp_bands
        rows = (sources % n_grp_bands)[:, None] == jnp.arange(n_grp_bands, dtype=jnp.int32)[None, :]
        picked = jnp.dot(rows.astype(jnp.float32), orbitals, precision=HI)
        picked = jnp.where((owner == g)[:, None], picked, 0.0)
        spread = jnp.broadcast_to(picked[None], (n_grp, n_src, width))
        picked = jnp.sum(lax.all_to_all(spread, "grp", 0, 0, tiled=True), axis=0)
        send = jnp.concatenate(
            [orbitals[:, None, :], jnp.broadcast_to(picked[None], (n_grp_bands, n_src, width))], axis=1)
        send, column_cell, column_length = lax.optimization_barrier((send, column_cell, column_length))
        got = lax.all_to_all(send, "col", 0, 0, tiled=True)
        table = cas_matrix(extent)
        kernel = kernel_grid(extent)
        cos_h, sin_h, live = shift_tables(column_length, depth, extent)
        slot = jnp.arange(depth, dtype=jnp.int32)
        fwd = jnp.concatenate([table[:depth], table[(extent - slot) % extent]], axis=1)
        bwd = jnp.concatenate([table[:, :depth], table[:, (extent - slot) % extent]], axis=0)
        w = lax.optimization_barrier(plane_matrix(column_cell, table, extent))
        n = 1 + n_src
        coeff = got.reshape(n_col, n, width // depth, depth).transpose(0, 2, 1, 3).reshape(count, n, depth)
        coeff = jnp.where(live[:, None, :], coeff, 0.0)
        both = jnp.dot(coeff.reshape(count * n, depth), fwd, precision=HI).reshape(count, n, 2, extent)
        cols = cos_h[:, None, :] * both[:, :, 0] - sin_h[:, None, :] * both[:, :, 1]
        grids = jnp.dot(w, cols.reshape(count, n * extent), precision=MID)
        grids = grids.reshape(extent, extent, n, extent)
        own = grids[:, :, :1]
        src = grids[:, :, 1:]
        density = own * src
        potential = cas_three_reversed(kernel[:, :, None, :] * cas_three(density, table), table)
        total = jnp.sum(weights[None, None, :, None] * potential * src, axis=2)
        back = lax.dot_general(w, total.reshape(extent * extent, extent), (((0,), (0,)), ((), ())), precision=MID)
        scaled = jnp.concatenate([back * cos_h, -(back * sin_h)], axis=1)
        out = -jnp.dot(scaled, bwd, precision=HI)
        out = jnp.where(live, out, 0.0)
        return lax.all_to_all(out.reshape(n_col, 1, width), "col", 0, 0, tiled=True).reshape(n_col, width)

    return local


def solution(mesh):
    n_grp = mesh.shape["grp"]
    n_col = mesh.shape["col"]

    def run(orbitals, column_cell, column_length, sources, weights):
        n_grp_bands = orbitals.shape[0] // n_grp
        body = make_local(n_grp_bands, n_grp, n_col)
        return jax.shard_map(
            body,
            mesh=mesh,
            in_specs=(P("grp", "col"), P(), P(), P(), P()),
            out_specs=P("grp", "col"),
            check_vma=False,
        )(orbitals, column_cell, column_length, sources, weights)

    return run
```
